256 devices in a mesh: dp: 32 (over x, z_hi, core), expert: 8 (over z_lo, y).
Axes of the slice: x: 4, y: 4, z: 8 (z_hi: 4, z_lo: 2; z = z_hi * 2 + z_lo), core: 2. Of those that a mesh axis runs over, the one named last changes fastest.
Arguments:
- tokens: bfloat16 [65536, 2560], P(('dp', 'expert')), may hold values from -24 to 24
- routes: int32 [65536, 1], P(('dp', 'expert')), may hold values from 0 to 7; in each aligned block of 256 rows (0 to 255, 256 to 511, ...) at most 40 rows name the same one
- gate_levels: int32 [65536, 1], P(('dp', 'expert')), may hold values from 1 to 64
- w_gate: bfloat16 [8, 2560, 768], P('expert', 'dp'), may hold values from -0.125 to 0.125
- w_up: bfloat16 [8, 2560, 768], P('expert', 'dp'), may hold values from -0.125 to 0.125
- w_down: bfloat16 [8, 2560, 768], P('expert', 'dp'), may hold values from -0.21875 to 0.21875
- grad_out: bfloat16 [65536, 2560], P(('dp', 'expert')), may hold values from -24 to 24
Outputs:
- moe_out: bfloat16 [65536, 2560], P(('dp', 'expert'))
- grad_tokens: bfloat16 [65536, 2560], P(('dp', 'expert'))
- grad_gate: float32 [8, 2560, 768], P('expert', 'dp')
- grad_up: float32 [8, 2560, 768], P('expert', 'dp')
- grad_down: float32 [8, 2560, 768], P('expert', 'dp')
The draws below stay inside these ranges and needn't reach their ends.
Inputs may be any that keep to these rules, and one draw needn't show every extreme that they name: `routes`: among the rows of one device, no expert is named by more than 40 tokens, a bound that some block reaches.
All inputs are finite; a program needn't handle non-finite values.
Results may differ from the reference program's by a relative error of at most 0.019.
Values may be sent and summed in bfloat16 or wider, within the bound.
No kernel may reach another device: no remote copies, remote signals or barrier semaphores. Data moves between devices by JAX's collectives and lax.ppermute only.
A program may use at most 128 MiB of HBM per device.

```python
import math
import jax
import jax.numpy as jnp
import numpy as np
from jax import lax

D = 2560
FF = 768
TOP = 1
TOK_DEV = 256
EXPERTS = 8
CAP = 40
TOKENS = 65536
N_DP = 32
N_EXPERT = 8


def place_ends(values, key, least, high):
    spot = [jax.random.randint(jax.random.fold_in(key, axis), (), 0, length) for axis, length in enumerate(values.shape)]
    widest = values.shape.index(max(values.shape))
    next_to = spot[:widest] + [(spot[widest] + 1) % values.shape[widest]] + spot[widest + 1:]
    return values.at[tuple(spot)].set(least).at[tuple(next_to)].set(high)


def with_spikes(array, rng, source, target, blocks, factor):
    owner, partner = [(jnp.arange(array.shape[dim]) // (array.shape[dim] // blocks)).reshape([-1 if axis == dim else 1 for axis in range(array.ndim)]) for dim in (source, target)]
    chosen = jax.random.permutation(rng, blocks)[partner]
    strong = (owner == chosen) | (owner == (partner + blocks // 2) % blocks)
    return jnp.where(strong, factor * array, array)


def shard_levels(key, extent, cuts, smallest, top_value):
    gain = 1.0
    for position, parts in cuts:
        heights = jax.random.uniform(jax.random.fold_in(jax.random.fold_in(key, 6), position), (parts,), jnp.float32, smallest / len(cuts), top_value / len(cuts))
        gain = gain * jnp.repeat(jnp.exp(heights), extent[position] // parts).reshape((-1,) + (1,) * (len(extent) - 1 - position))
    return gain


def deal_out(own_key, own, number, rows, count, top, most, slope):
    ranking = jax.random.permutation(own_key, count)
    packed, ordinary = portions_of(count, rows * top, most, slope, True), portions_of(count, rows * top, most, slope, False)
    places = jnp.arange(count)

    def named(sizes, turn):
        used = int((sizes > 0).sum())
        fixed = max(1, used // 4)
        passed = fixed + (places - fixed + turn * (used - fixed)) % max(1, count - fixed)
        return jnp.zeros((count,), jnp.int32).at[ranking[jnp.where(places < fixed, places, passed)]].set(jnp.asarray(sizes, jnp.int32))

    sizes = jnp.where(number % 4 == 0, named(packed, number // 4), named(ordinary, number - number // 4 - 1))
    mixed = jax.random.permutation(jax.random.fold_in(own, 3), count)
    donor, sink = mixed[0:count // 2 * 2:2], mixed[1:count // 2 * 2:2]
    margin = jnp.minimum(sizes[donor] - 1, most - sizes[sink]) // 2
    margin = jnp.where((donor == ranking[0]) | (sink == ranking[0]) | (sizes[sink] == 0), 0, jnp.maximum(margin, 0))
    passed = jax.random.randint(jax.random.fold_in(own, 4), (count // 2,), 0, 1 << 20) % (margin + 1)
    sizes = sizes.at[donor].add(-passed).at[sink].add(passed)
    labels = jnp.searchsorted(jnp.cumsum(sizes), jnp.arange(rows * top), side="right").astype(jnp.int32)
    grid = labels.reshape(top, rows).T
    grid = grid[jax.random.permutation(jax.random.fold_in(own, 1), rows)]
    turn = jax.random.randint(jax.random.fold_in(own, 2), (rows, 1), 0, top)
    return jnp.take_along_axis(grid, (jnp.arange(top)[None, :] + turn) % top, axis=1)


def portions_of(amount, total, limit, lean, full):
    loads = [(1 << 20) // math.isqrt(grade ** lean) + 1 for grade in range(1, amount + 1)]
    largest = limit if full else min(limit, max(-(-total // amount), total * loads[0] // sum(loads)))
    least = 1 if total - largest >= amount - 1 else 0
    given, surplus = [largest] + [least] * (amount - 1), total - largest - least * (amount - 1)
    while surplus > 0:
        movable = [i for i in range(1, amount) if given[i] < largest] or [i for i in range(1, amount) if given[i] < limit]
        pool, remaining = sum([loads[i] for i in movable]), surplus
        for i in movable:
            extra = min(limit - given[i], max(1, remaining * loads[i] // pool), surplus)
            given[i] = given[i] + extra
            surplus = surplus - extra
    return np.array(given)


def centred(stream_key, extent, scale, reach, cuts=(), held_as=jnp.bfloat16):
    gain = shard_levels(stream_key, extent, cuts, -0.22, 0.18) if cuts else 1.0
    values = jax.random.normal(stream_key, extent, jnp.float32) * scale * gain
    return jnp.minimum(jnp.maximum(values, -reach), reach).astype(held_as)


def heavy_noise(rng, shape, deviation, limit, shards, heavy, kind=jnp.bfloat16):
    entries = deviation * jax.random.normal(rng, shape, jnp.float32)
    if shards:
        entries = entries * shard_levels(rng, shape, shards, -0.22, 0.18)
    return jnp.clip(with_spikes(entries, jax.random.fold_in(rng, 3), *heavy), -limit, limit).astype(kind)


def setup_inputs(seed: int = 0) -> dict:
    key_of = jax.random.split(jax.random.key(seed), 8)
    tokens = heavy_noise(key_of[0], (TOKENS, D), 1.0, 24.0, ((0, 256),), (0, 1, 256, 6.0))
    routes_keys = jax.random.split(jax.random.fold_in(key_of[1], 1), TOKENS // TOK_DEV)
    routes_turns = jax.random.permutation(jax.random.fold_in(key_of[1], 3), TOKENS // TOK_DEV)
    routes = jax.vmap(lambda own, number: deal_out(jax.random.fold_in(key_of[1], 2), own, number, TOK_DEV, EXPERTS, TOP, CAP, 2))(routes_keys, routes_turns).reshape((TOKENS, TOP))
    gate_levels = place_ends(jax.random.randint(key_of[2], (TOKENS, TOP), 1, 65), jax.random.fold_in(key_of[2], 1), 1, 64).astype(jnp.int32)
    w_gate = centred(key_of[3], (EXPERTS, D, FF), D ** -0.5, 0.125, ((0, 8), (1, 32)))
    w_up = centred(key_of[4], (EXPERTS, D, FF), D ** -0.5, 0.125, ((0, 8), (1, 32)))
    w_down = centred(key_of[5], (EXPERTS, D, FF), FF ** -0.5, 0.21875, ((0, 8), (1, 32)))
    grad_out = heavy_noise(key_of[6], (TOKENS, D), 1.0, 24.0, ((0, 256),), (0, 1, 256, 6.0))
    return {"tokens": tokens, "routes": routes, "gate_levels": gate_levels, "w_gate": w_gate, "w_up": w_up, "w_down": w_down, "grad_out": grad_out}


def contract_last(matrix_a, matrix_b):
    return lax.dot_general(matrix_a, matrix_b, (((1,), (1,)), ((), ())), preferred_element_type=jnp.float32)


def contract_first(matrix_a, matrix_b):
    return lax.dot_general(matrix_a, matrix_b, (((0,), (0,)), ((), ())), preferred_element_type=jnp.float32)


def block_ranks(expert_of):
    onehot = (expert_of[:, None] == jnp.arange(EXPERTS, dtype=jnp.int32)[None, :]).astype(jnp.int32)
    earlier = jnp.cumsum(onehot, axis=0) - onehot
    return jnp.sum(earlier * onehot, axis=1).astype(jnp.int32)


def place_rows(values, expert_of, slot_rank):
    return jnp.zeros((EXPERTS, CAP, D), jnp.bfloat16).at[expert_of, slot_rank].set(values)


def pick_rows(stacked, expert_of, slot_rank):
    return stacked[expert_of, slot_rank]


def expert_pass(received, grad_rows, gate_full, up_full, down_full):
    act_gate = jnp.dot(received, gate_full, preferred_element_type=jnp.float32)
    act_up = jnp.dot(received, up_full, preferred_element_type=jnp.float32)
    sigmoid_gate = jax.nn.sigmoid(act_gate)
    silu_gate = act_gate * sigmoid_gate
    hidden = (silu_gate * act_up).astype(jnp.bfloat16)
    expert_out = contract_last(hidden, down_full).astype(jnp.bfloat16)
    hidden_grad = jnp.dot(grad_rows, down_full, preferred_element_type=jnp.float32)
    gate_delta = (hidden_grad * act_up * sigmoid_gate * (1.0 + act_gate * (1.0 - sigmoid_gate))).astype(jnp.bfloat16)
    up_delta = (hidden_grad * silu_gate).astype(jnp.bfloat16)
    token_grad = (contract_last(gate_delta, gate_full) + contract_last(up_delta, up_full)).astype(jnp.bfloat16)
    part_gate = contract_first(received, gate_delta).astype(jnp.bfloat16)
    part_up = contract_first(received, up_delta).astype(jnp.bfloat16)
    part_down = contract_first(grad_rows, hidden).astype(jnp.bfloat16)
    return expert_out, token_grad, part_gate, part_up, part_down


def reference(tokens, routes, gate_levels, w_gate, w_up, w_down, grad_out):
    tok_blocks = tokens.reshape(N_DP, N_EXPERT, TOK_DEV, D)
    route_blocks = routes.reshape(N_DP, N_EXPERT, TOK_DEV)
    level_blocks = gate_levels.reshape(N_DP, N_EXPERT, TOK_DEV, 1)
    grad_blocks = grad_out.reshape(N_DP, N_EXPERT, TOK_DEV, D)

    def row_pass(carry, inputs):
        tok_row, route_row, level_row, grad_row = inputs
        rank_row = jax.vmap(block_ranks)(route_row)
        gate_weight = level_row.astype(jnp.float32) / 64.0
        out_grad = (gate_weight * grad_row.astype(jnp.float32)).astype(jnp.bfloat16)
        tok_place = jax.vmap(place_rows)(tok_row, route_row, rank_row)
        grad_place = jax.vmap(place_rows)(out_grad, route_row, rank_row)
        outs_list = []
        grads_list = []
        gate_parts = []
        up_parts = []
        down_parts = []
        for expert in range(EXPERTS):
            received = tok_place[:, expert].reshape(N_EXPERT * CAP, D)
            grad_rows = grad_place[:, expert].reshape(N_EXPERT * CAP, D)
            results = expert_pass(received, grad_rows, w_gate[expert], w_up[expert], w_down[expert])
            outs_list.append(results[0].reshape(N_EXPERT, CAP, D))
            grads_list.append(results[1].reshape(N_EXPERT, CAP, D))
            gate_parts.append(results[2])
            up_parts.append(results[3])
            down_parts.append(results[4])
        out_stack = jnp.stack(outs_list, axis=1)
        grad_stack = jnp.stack(grads_list, axis=1)
        expert_out = jax.vmap(pick_rows)(out_stack, route_row, rank_row)
        moe_row = (gate_weight * expert_out.astype(jnp.float32)).astype(jnp.bfloat16)
        grad_row_out = jax.vmap(pick_rows)(grad_stack, route_row, rank_row)
        new_carry = (carry[0] + jnp.stack(gate_parts).astype(jnp.float32),
                     carry[1] + jnp.stack(up_parts).astype(jnp.float32),
                     carry[2] + jnp.stack(down_parts).astype(jnp.float32))
        return new_carry, (moe_row, grad_row_out)

    zeros = jnp.zeros((EXPERTS, D, FF), jnp.float32)
    sums, rows_out = lax.scan(row_pass, (zeros, zeros, zeros), (tok_blocks, route_blocks, level_blocks, grad_blocks))
    moe_out = rows_out[0].reshape(TOKENS, D)
    grad_tokens = rows_out[1].reshape(TOKENS, D)
    return moe_out, grad_tokens, sums[0], sums[1], sums[2]
```

```python
import jax
import jax.numpy as jnp
from jax import lax
from jax.sharding import Mesh
from jax.sharding import PartitionSpec as P

TOP = 1
CHIPS = ("x", "zh")
DP = ("x", "zh", "core")


def contract_last(matrix_a, matrix_b):
    return lax.dot_general(
        matrix_a, matrix_b, (((1,), (1,)), ((), ())), preferred_element_type=jnp.float32
    )


def contract_first(matrix_a, matrix_b):
    return lax.dot_general(
        matrix_a, matrix_b, (((0,), (0,)), ((), ())), preferred_element_type=jnp.float32
    )


def swap_cores(value):
    return lax.ppermute(value, "core", perm=[(0, 1), (1, 0)])


def gather_weight(weight):
    own = lax.all_to_all(weight, "core", split_axis=1, concat_axis=0, tiled=True)
    own = lax.all_gather(own, CHIPS, axis=0, tiled=True)
    other = swap_cores(own)
    return jnp.concatenate([own, other], axis=1)


def scatter_grad(part):
    half = part.shape[1] // 2
    rounded = part.astype(jnp.bfloat16)
    arrived = swap_cores(rounded[:, half:])
    pair_sum = (rounded[:, :half].astype(jnp.float32) + arrived.astype(jnp.float32)).astype(
        jnp.bfloat16
    )
    chip_sum = lax.psum_scatter(pair_sum, CHIPS, scatter_dimension=0, tiled=True)
    block = lax.all_to_all(chip_sum, "core", split_axis=0, concat_axis=1, tiled=True)
    return block.astype(jnp.float32)


def shards(tokens, routes, gate_levels, w_gate, w_up, w_down, grad_out):
    experts = lax.axis_size("expert")
    tok_rows = tokens.shape[0]
    model_width = tokens.shape[1]
    capacity = min(tok_rows, tok_rows * TOP * 5 // (4 * experts))
    slot_count = experts * capacity
    expert_of = routes[:, 0]
    onehot = (expert_of[:, None] == jnp.arange(experts, dtype=jnp.int32)[None, :]).astype(jnp.int32)
    earlier = jnp.cumsum(onehot, axis=0) - onehot
    slot_rank = jnp.sum(earlier * onehot, axis=1)
    slot_index = expert_of * capacity + slot_rank
    source_row = (
        jnp.zeros((slot_count,), jnp.int32)
        .at[slot_index]
        .set(jnp.arange(tok_rows, dtype=jnp.int32))
    )
    filled = (
        jnp.zeros((slot_count, 1), jnp.bfloat16)
        .at[slot_index, 0]
        .set(jnp.ones((tok_rows,), jnp.bfloat16))
    )
    gate_weight = gate_levels.astype(jnp.float32) / 64.0

    def pack_rows(values):
        return (jnp.take(values, source_row, axis=0) * filled).reshape(
            experts, capacity, model_width
        )

    gate_full = gather_weight(w_gate[0])
    up_full = gather_weight(w_up[0])
    down_full = gather_weight(w_down[0])
    received = lax.all_to_all(
        pack_rows(tokens), "expert", split_axis=0, concat_axis=0, tiled=True
    ).reshape(slot_count, model_width)
    act_gate = jnp.dot(received, gate_full, preferred_element_type=jnp.float32)
    act_up = jnp.dot(received, up_full, preferred_element_type=jnp.float32)
    sigmoid_gate = jax.nn.sigmoid(act_gate)
    silu_gate = act_gate * sigmoid_gate
    hidden = (silu_gate * act_up).astype(jnp.bfloat16)
    expert_out = (
        contract_last(hidden, down_full)
        .astype(jnp.bfloat16)
        .reshape(experts, capacity, model_width)
    )
    returned = lax.all_to_all(
        expert_out, "expert", split_axis=0, concat_axis=0, tiled=True
    ).reshape(slot_count, model_width)
    moe_out = (gate_weight * jnp.take(returned, slot_index, axis=0).astype(jnp.float32)).astype(
        jnp.bfloat16
    )
    out_grad = (gate_weight * grad_out.astype(jnp.float32)).astype(jnp.bfloat16)
    grad_rows = lax.all_to_all(
        pack_rows(out_grad), "expert", split_axis=0, concat_axis=0, tiled=True
    ).reshape(slot_count, model_width)
    hidden_grad = jnp.dot(grad_rows, down_full, preferred_element_type=jnp.float32)
    gate_delta = (
        hidden_grad * act_up * sigmoid_gate * (1.0 + act_gate * (1.0 - sigmoid_gate))
    ).astype(jnp.bfloat16)
    up_delta = (hidden_grad * silu_gate).astype(jnp.bfloat16)
    token_grad = (contract_last(gate_delta, gate_full) + contract_last(up_delta, up_full)).astype(
        jnp.bfloat16
    )
    arrived = lax.all_to_all(
        token_grad.reshape(experts, capacity, model_width),
        "expert",
        split_axis=0,
        concat_axis=0,
        tiled=True,
    )
    grad_tokens = jnp.take(arrived.reshape(slot_count, model_width), slot_index, axis=0)
    grad_down = scatter_grad(contract_first(grad_rows, hidden))
    grad_gate = scatter_grad(contract_first(received, gate_delta))
    grad_up = scatter_grad(contract_first(received, up_delta))
    return (moe_out, grad_tokens, grad_gate[None], grad_up[None], grad_down[None])


def solution(mesh):
    dp_size, expert_size = mesh.devices.shape
    chips = dp_size // 2
    x_size = 4 if chips % 4 == 0 else 1
    grid = mesh.devices.reshape(x_size, chips // x_size, 2, expert_size)
    fine = Mesh(grid, DP + ("expert",))
    rows = P(DP + ("expert",), None)
    weights = P("expert", DP, None)
    in_specs = (rows, rows, rows, weights, weights, weights, rows)
    out_specs = (rows, rows, weights, weights, weights)
    return jax.shard_map(shards, mesh=fine, in_specs=in_specs, out_specs=out_specs, check_vma=False)
```

```python
import jax
import jax.numpy as jnp
from jax import lax
from jax.sharding import Mesh
from jax.sharding import PartitionSpec as P

TOP = 1
CHIPS = ("x", "zh")
DP = ("x", "zh", "core")


def contract_last(matrix_a, matrix_b):
    return lax.dot_general(
        matrix_a, matrix_b, (((1,), (1,)), ((), ())), preferred_element_type=jnp.float32
    )


def contract_first(matrix_a, matrix_b):
    return lax.dot_general(
        matrix_a, matrix_b, (((0,), (0,)), ((), ())), preferred_element_type=jnp.float32
    )


def swap_cores(value):
    return lax.ppermute(value, "core", perm=[(0, 1), (1, 0)])


def gather_weights(*weights):
    stacked = jnp.stack(weights)
    own = lax.all_to_all(stacked, "core", split_axis=2, concat_axis=1, tiled=True)
    own = lax.all_gather(own, CHIPS, axis=1, tiled=True)
    other = swap_cores(own)
    return [(own[i], other[i]) for i in range(len(weights))]


def scatter_grads(*parts):
    own = jnp.stack([p[0] for p in parts]).astype(jnp.bfloat16)
    other = jnp.stack([p[1] for p in parts]).astype(jnp.bfloat16)
    arrived = swap_cores(other)
    pair_sum = (own.astype(jnp.float32) + arrived.astype(jnp.float32)).astype(jnp.bfloat16)
    chip_sum = lax.psum_scatter(pair_sum, CHIPS, scatter_dimension=1, tiled=True)
    block = lax.all_to_all(chip_sum, "core", split_axis=1, concat_axis=2, tiled=True)
    block = block.astype(jnp.float32)
    return [block[i] for i in range(len(parts))]


def halves(left, pair, dims):
    return (
        lax.dot_general(left, pair[0], dims, preferred_element_type=jnp.float32),
        lax.dot_general(left, pair[1], dims, preferred_element_type=jnp.float32),
    )


def shards(tokens, routes, gate_levels, w_gate, w_up, w_down, grad_out):
    experts = lax.axis_size("expert")
    tok_rows = tokens.shape[0]
    model_width = tokens.shape[1]
    capacity = min(tok_rows, tok_rows * TOP * 5 // (4 * experts))
    slot_count = experts * capacity
    expert_of = routes[:, 0]
    onehot = (expert_of[:, None] == jnp.arange(experts, dtype=jnp.int32)[None, :]).astype(jnp.int32)
    earlier = jnp.cumsum(onehot, axis=0) - onehot
    slot_rank = jnp.sum(earlier * onehot, axis=1)
    slot_index = expert_of * capacity + slot_rank
    source_row = (
        jnp.zeros((slot_count,), jnp.int32)
        .at[slot_index]
        .set(jnp.arange(tok_rows, dtype=jnp.int32))
    )
    filled = (
        jnp.zeros((slot_count, 1), jnp.bfloat16)
        .at[slot_index, 0]
        .set(jnp.ones((tok_rows,), jnp.bfloat16))
    )
    gate_weight = gate_levels.astype(jnp.float32) / 64.0

    def pack_rows(values):
        return (jnp.take(values, source_row, axis=0) * filled).reshape(
            experts, capacity, model_width
        )

    gate_pair, up_pair, down_pair = gather_weights(w_gate[0], w_up[0], w_down[0])
    plain = (((1,), (0,)), ((), ()))
    last = (((1,), (1,)), ((), ()))
    received = lax.all_to_all(
        pack_rows(tokens), "expert", split_axis=0, concat_axis=0, tiled=True
    ).reshape(slot_count, model_width)
    act_gate = jnp.concatenate(halves(received, gate_pair, plain), axis=1)
    act_up = jnp.concatenate(halves(received, up_pair, plain), axis=1)
    sigmoid_gate = jax.nn.sigmoid(act_gate)
    silu_gate = act_gate * sigmoid_gate
    hidden = (silu_gate * act_up).astype(jnp.bfloat16)
    half = hidden.shape[1] // 2
    expert_out = (
        (
            contract_last(hidden[:, :half], down_pair[0])
            + contract_last(hidden[:, half:], down_pair[1])
        )
        .astype(jnp.bfloat16)
        .reshape(experts, capacity, model_width)
    )
    returned = lax.all_to_all(
        expert_out, "expert", split_axis=0, concat_axis=0, tiled=True
    ).reshape(slot_count, model_width)
    moe_out = (gate_weight * jnp.take(returned, slot_index, axis=0).astype(jnp.float32)).astype(
        jnp.bfloat16
    )
    out_grad = (gate_weight * grad_out.astype(jnp.float32)).astype(jnp.bfloat16)
    grad_rows = lax.all_to_all(
        pack_rows(out_grad), "expert", split_axis=0, concat_axis=0, tiled=True
    ).reshape(slot_count, model_width)
    hidden_grad = jnp.concatenate(halves(grad_rows, down_pair, plain), axis=1)
    gate_delta = (
        hidden_grad * act_up * sigmoid_gate * (1.0 + act_gate * (1.0 - sigmoid_gate))
    ).astype(jnp.bfloat16)
    up_delta = (hidden_grad * silu_gate).astype(jnp.bfloat16)
    token_grad = (
        contract_last(gate_delta[:, :half], gate_pair[0])
        + contract_last(gate_delta[:, half:], gate_pair[1])
        + contract_last(up_delta[:, :half], up_pair[0])
        + contract_last(up_delta[:, half:], up_pair[1])
    ).astype(jnp.bfloat16)
    arrived = lax.all_to_all(
        token_grad.reshape(experts, capacity, model_width),
        "expert",
        split_axis=0,
        concat_axis=0,
        tiled=True,
    )
    grad_tokens = jnp.take(arrived.reshape(slot_count, model_width), slot_index, axis=0)
    grad_gate, grad_up, grad_down = scatter_grads(
        (contract_first(received, gate_delta[:, :half]), contract_first(received, gate_delta[:, half:])),
        (contract_first(received, up_delta[:, :half]), contract_first(received, up_delta[:, half:])),
        (contract_first(grad_rows, hidden[:, :half]), contract_first(grad_rows, hidden[:, half:])),
    )
    return (moe_out, grad_tokens, grad_gate[None], grad_up[None], grad_down[None])


def solution(mesh):
    dp_size, expert_size = mesh.devices.shape
    chips = dp_size // 2
    x_size = 4 if chips % 4 == 0 else 1
    grid = mesh.devices.reshape(x_size, chips // x_size, 2, expert_size)
    fine = Mesh(grid, DP + ("expert",))
    rows = P(DP + ("expert",), None)
    weights = P("expert", DP, None)
    in_specs = (rows, rows, rows, weights, weights, weights, rows)
    out_specs = (rows, rows, weights, weights, weights)
    return jax.shard_map(shards, mesh=fine, in_specs=in_specs, out_specs=out_specs, check_vma=False)
```

```python
import jax
import jax.numpy as jnp
from jax import lax
from jax.sharding import Mesh
from jax.sharding import PartitionSpec as P

TOP = 1
CHIPS = ("x", "zh")
DP = ("x", "zh", "core")


def contract_last(matrix_a, matrix_b):
    return lax.dot_general(
        matrix_a, matrix_b, (((1,), (1,)), ((), ())), preferred_element_type=jnp.float32
    )


def contract_first(matrix_a, matrix_b):
    return lax.dot_general(
        matrix_a, matrix_b, (((0,), (0,)), ((), ())), preferred_element_type=jnp.float32
    )


def swap_cores(value):
    return lax.ppermute(value, "core", perm=[(0, 1), (1, 0)])


def gather_weights(*weights):
    stacked = jnp.stack(weights)
    own = lax.all_to_all(stacked, "core", split_axis=2, concat_axis=1, tiled=True)
    own = lax.all_gather(own, CHIPS, axis=1, tiled=True)
    other = swap_cores(own)
    return [(own[i], other[i]) for i in range(len(weights))]


def scatter_grads(*parts):
    core = lax.axis_index("core")
    stacked = jnp.stack(parts).astype(jnp.bfloat16)
    count, width, ff = stacked.shape
    chips = lax.axis_size(CHIPS)
    grouped = stacked.reshape(count, chips, 2, width // (2 * chips), ff)
    mine = lax.dynamic_index_in_dim(grouped, core, axis=2, keepdims=False)
    theirs = lax.dynamic_index_in_dim(grouped, 1 - core, axis=2, keepdims=False)
    arrived = swap_cores(theirs)
    pair_sum = (mine.astype(jnp.float32) + arrived.astype(jnp.float32)).astype(jnp.bfloat16)
    pair_sum = pair_sum.reshape(count, width // 2, ff)
    block = lax.psum_scatter(pair_sum, CHIPS, scatter_dimension=1, tiled=True)
    block = block.astype(jnp.float32)
    return [block[i] for i in range(count)]


def true_order(value):
    core = lax.axis_index("core")
    half = value.shape[1] // 2
    both = jnp.concatenate([value, value], axis=1)
    return lax.dynamic_slice_in_dim(both, core * half, 2 * half, axis=1)


def halves(left, pair, dims):
    return (
        lax.dot_general(left, pair[0], dims, preferred_element_type=jnp.float32),
        lax.dot_general(left, pair[1], dims, preferred_element_type=jnp.float32),
    )


def shards(tokens, routes, gate_levels, w_gate, w_up, w_down, grad_out):
    experts = lax.axis_size("expert")
    tok_rows = tokens.shape[0]
    model_width = tokens.shape[1]
    capacity = min(tok_rows, tok_rows * TOP * 5 // (4 * experts))
    slot_count = experts * capacity
    expert_of = routes[:, 0]
    onehot = (expert_of[:, None] == jnp.arange(experts, dtype=jnp.int32)[None, :]).astype(jnp.int32)
    earlier = jnp.cumsum(onehot, axis=0) - onehot
    slot_rank = jnp.sum(earlier * onehot, axis=1)
    slot_index = expert_of * capacity + slot_rank
    source_row = (
        jnp.zeros((slot_count,), jnp.int32)
        .at[slot_index]
        .set(jnp.arange(tok_rows, dtype=jnp.int32))
    )
    filled = (
        jnp.zeros((slot_count, 1), jnp.bfloat16)
        .at[slot_index, 0]
        .set(jnp.ones((tok_rows,), jnp.bfloat16))
    )
    gate_weight = gate_levels.astype(jnp.float32) / 64.0

    def pack_rows(values):
        return (jnp.take(values, source_row, axis=0) * filled).reshape(
            experts, capacity, model_width
        )

    gate_pair, up_pair, down_pair = gather_weights(w_gate[0], w_up[0], w_down[0])
    plain = (((1,), (0,)), ((), ()))
    last = (((1,), (1,)), ((), ()))
    out_grad = (gate_weight * grad_out.astype(jnp.float32)).astype(jnp.bfloat16)
    both_rows = lax.all_to_all(
        jnp.stack([pack_rows(tokens), pack_rows(out_grad)]),
        "expert",
        split_axis=1,
        concat_axis=1,
        tiled=True,
    )
    received = both_rows[0].reshape(slot_count, model_width)
    grad_rows = both_rows[1].reshape(slot_count, model_width)
    act_gate = jnp.concatenate(halves(received, gate_pair, plain), axis=1)
    act_up = jnp.concatenate(halves(received, up_pair, plain), axis=1)
    sigmoid_gate = jax.nn.sigmoid(act_gate)
    silu_gate = act_gate * sigmoid_gate
    hidden = (silu_gate * act_up).astype(jnp.bfloat16)
    half = hidden.shape[1] // 2
    expert_out = (
        (
            contract_last(hidden[:, :half], down_pair[0])
            + contract_last(hidden[:, half:], down_pair[1])
        )
        .astype(jnp.bfloat16)
        .reshape(experts, capacity, model_width)
    )
    returned = lax.all_to_all(
        expert_out, "expert", split_axis=0, concat_axis=0, tiled=True
    ).reshape(slot_count, model_width)
    moe_out = (gate_weight * jnp.take(returned, slot_index, axis=0).astype(jnp.float32)).astype(
        jnp.bfloat16
    )
    hidden_grad = jnp.concatenate(halves(grad_rows, down_pair, plain), axis=1)
    gate_delta = (
        hidden_grad * act_up * sigmoid_gate * (1.0 + act_gate * (1.0 - sigmoid_gate))
    ).astype(jnp.bfloat16)
    up_delta = (hidden_grad * silu_gate).astype(jnp.bfloat16)
    token_grad = (
        contract_last(gate_delta[:, :half], gate_pair[0])
        + contract_last(gate_delta[:, half:], gate_pair[1])
        + contract_last(up_delta[:, :half], up_pair[0])
        + contract_last(up_delta[:, half:], up_pair[1])
    ).astype(jnp.bfloat16)
    arrived = lax.all_to_all(
        token_grad.reshape(experts, capacity, model_width),
        "expert",
        split_axis=0,
        concat_axis=0,
        tiled=True,
    )
    grad_tokens = jnp.take(arrived.reshape(slot_count, model_width), slot_index, axis=0)
    grad_gate, grad_up, grad_down = scatter_grads(
        contract_first(received, true_order(gate_delta)),
        contract_first(received, true_order(up_delta)),
        contract_first(grad_rows, true_order(hidden)),
    )
    return (moe_out, grad_tokens, grad_gate[None], grad_up[None], grad_down[None])


def solution(mesh):
    dp_size, expert_size = mesh.devices.shape
    chips = dp_size // 2
    x_size = 4 if chips % 4 == 0 else 1
    grid = mesh.devices.reshape(x_size, chips // x_size, 2, expert_size)
    fine = Mesh(grid, DP + ("expert",))
    rows = P(DP + ("expert",), None)
    weights = P("expert", DP, None)
    in_specs = (rows, rows, rows, weights, weights, weights, rows)
    out_specs = (rows, rows, weights, weights, weights)
    return jax.shard_map(shards, mesh=fine, in_specs=in_specs, out_specs=out_specs, check_vma=False)
```

```python
import jax
import jax.numpy as jnp
from jax import lax
from jax.sharding import Mesh
from jax.sharding import PartitionSpec as P

TOP = 1
CHIPS = ("x", "zh")
DP = ("x", "zh", "core")


def contract_last(matrix_a, matrix_b):
    return lax.dot_general(
        matrix_a, matrix_b, (((1,), (1,)), ((), ())), preferred_element_type=jnp.float32
    )


def contract_first(matrix_a, matrix_b):
    return lax.dot_general(
        matrix_a, matrix_b, (((0,), (0,)), ((), ())), preferred_element_type=jnp.float32
    )


def swap_cores(value):
    return lax.ppermute(value, "core", perm=[(0, 1), (1, 0)])


def gather_weights(*weights):
    stacked = jnp.stack(weights)
    own = lax.all_to_all(stacked, "core", split_axis=2, concat_axis=1, tiled=True)
    own = lax.all_gather(own, CHIPS, axis=1, tiled=True)
    other = swap_cores(own)
    return [(own[i], other[i]) for i in range(len(weights))]


def owned_columns(rows):
    core = lax.axis_index("core")
    slots, width = rows.shape
    chips = lax.axis_size(CHIPS)
    grouped = rows.reshape(slots, chips, 2, width // (2 * chips))
    mine = lax.dynamic_index_in_dim(grouped, core, axis=2, keepdims=False)
    theirs = lax.dynamic_index_in_dim(grouped, 1 - core, axis=2, keepdims=False)
    return mine.reshape(slots, width // 2), theirs.reshape(slots, width // 2)


def scatter_grad(mine, theirs):
    arrived = swap_cores(theirs.astype(jnp.bfloat16))
    pair_sum = (
        mine.astype(jnp.bfloat16).astype(jnp.float32) + arrived.astype(jnp.float32)
    ).astype(jnp.bfloat16)
    return pair_sum


def true_order(value):
    core = lax.axis_index("core")
    half = value.shape[1] // 2
    both = jnp.concatenate([value, value], axis=1)
    return lax.dynamic_slice_in_dim(both, core * half, 2 * half, axis=1)


def halves(left, pair, dims):
    return (
        lax.dot_general(left, pair[0], dims, preferred_element_type=jnp.float32),
        lax.dot_general(left, pair[1], dims, preferred_element_type=jnp.float32),
    )


def shards(tokens, routes, gate_levels, w_gate, w_up, w_down, grad_out):
    experts = lax.axis_size("expert")
    tok_rows = tokens.shape[0]
    model_width = tokens.shape[1]
    capacity = min(tok_rows, tok_rows * TOP * 5 // (4 * experts))
    slot_count = experts * capacity
    expert_of = routes[:, 0]
    onehot = (expert_of[:, None] == jnp.arange(experts, dtype=jnp.int32)[None, :]).astype(jnp.int32)
    earlier = jnp.cumsum(onehot, axis=0) - onehot
    slot_rank = jnp.sum(earlier * onehot, axis=1)
    slot_index = expert_of * capacity + slot_rank
    source_row = (
        jnp.zeros((slot_count,), jnp.int32)
        .at[slot_index]
        .set(jnp.arange(tok_rows, dtype=jnp.int32))
    )
    filled = (
        jnp.zeros((slot_count, 1), jnp.bfloat16)
        .at[slot_index, 0]
        .set(jnp.ones((tok_rows,), jnp.bfloat16))
    )
    gate_weight = gate_levels.astype(jnp.float32) / 64.0

    def pack_rows(values):
        return (jnp.take(values, source_row, axis=0) * filled).reshape(
            experts, capacity, model_width
        )

    gate_pair, up_pair, down_pair = gather_weights(w_gate[0], w_up[0], w_down[0])
    plain = (((1,), (0,)), ((), ()))
    last = (((1,), (1,)), ((), ()))
    received = lax.all_to_all(
        pack_rows(tokens), "expert", split_axis=0, concat_axis=0, tiled=True
    ).reshape(slot_count, model_width)
    act_gate = jnp.concatenate(halves(received, gate_pair, plain), axis=1)
    act_up = jnp.concatenate(halves(received, up_pair, plain), axis=1)
    sigmoid_gate = jax.nn.sigmoid(act_gate)
    silu_gate = act_gate * sigmoid_gate
    hidden = (silu_gate * act_up).astype(jnp.bfloat16)
    half = hidden.shape[1] // 2
    expert_out = (
        (
            contract_last(hidden[:, :half], down_pair[0])
            + contract_last(hidden[:, half:], down_pair[1])
        )
        .astype(jnp.bfloat16)
        .reshape(experts, capacity, model_width)
    )
    returned = lax.all_to_all(
        expert_out, "expert", split_axis=0, concat_axis=0, tiled=True
    ).reshape(slot_count, model_width)
    moe_out = (gate_weight * jnp.take(returned, slot_index, axis=0).astype(jnp.float32)).astype(
        jnp.bfloat16
    )
    out_grad = (gate_weight * grad_out.astype(jnp.float32)).astype(jnp.bfloat16)
    grad_rows = lax.all_to_all(
        pack_rows(out_grad), "expert", split_axis=0, concat_axis=0, tiled=True
    ).reshape(slot_count, model_width)
    hidden_grad = jnp.concatenate(halves(grad_rows, down_pair, plain), axis=1)
    gate_delta = (
        hidden_grad * act_up * sigmoid_gate * (1.0 + act_gate * (1.0 - sigmoid_gate))
    ).astype(jnp.bfloat16)
    up_delta = (hidden_grad * silu_gate).astype(jnp.bfloat16)
    token_grad = (
        contract_last(gate_delta[:, :half], gate_pair[0])
        + contract_last(gate_delta[:, half:], gate_pair[1])
        + contract_last(up_delta[:, :half], up_pair[0])
        + contract_last(up_delta[:, half:], up_pair[1])
    ).astype(jnp.bfloat16)
    arrived = lax.all_to_all(
        token_grad.reshape(experts, capacity, model_width),
        "expert",
        split_axis=0,
        concat_axis=0,
        tiled=True,
    )
    grad_tokens = jnp.take(arrived.reshape(slot_count, model_width), slot_index, axis=0)
    recv_mine, recv_theirs = owned_columns(received)
    grad_mine, grad_theirs = owned_columns(grad_rows)
    pair_sums = []
    for left_mine, left_theirs, right in (
        (grad_mine, grad_theirs, true_order(hidden)),
        (recv_mine, recv_theirs, true_order(gate_delta)),
        (recv_mine, recv_theirs, true_order(up_delta)),
    ):
        pair_sums.append(
            scatter_grad(contract_first(left_mine, right), contract_first(left_theirs, right))
        )
    blocks = lax.psum_scatter(jnp.stack(pair_sums), CHIPS, scatter_dimension=1, tiled=True)
    blocks = blocks.astype(jnp.float32)
    grad_down, grad_gate, grad_up = blocks[0], blocks[1], blocks[2]
    return (moe_out, grad_tokens, grad_gate[None], grad_up[None], grad_down[None])


def solution(mesh):
    dp_size, expert_size = mesh.devices.shape
    chips = dp_size // 2
    x_size = 4 if chips % 4 == 0 else 1
    grid = mesh.devices.reshape(x_size, chips // x_size, 2, expert_size)
    fine = Mesh(grid, DP + ("expert",))
    rows = P(DP + ("expert",), None)
    weights = P("expert", DP, None)
    in_specs = (rows, rows, rows, weights, weights, weights, rows)
    out_specs = (rows, rows, weights, weights, weights)
    return jax.shard_map(shards, mesh=fine, in_specs=in_specs, out_specs=out_specs, check_vma=False)
```

```python
import jax
import jax.numpy as jnp
from jax import lax
from jax.sharding import Mesh
from jax.sharding import PartitionSpec as P

TOP = 1
CHIPS = ("x", "zh")
DP = ("x", "zh", "core")


def contract_last(matrix_a, matrix_b):
    return lax.dot_general(
        matrix_a, matrix_b, (((1,), (1,)), ((), ())), preferred_element_type=jnp.float32
    )


def contract_first(matrix_a, matrix_b):
    return lax.dot_general(
        matrix_a, matrix_b, (((0,), (0,)), ((), ())), preferred_element_type=jnp.float32
    )


def swap_cores(value):
    return lax.ppermute(value, "core", perm=[(0, 1), (1, 0)])


def gather_weights(*weights):
    stacked = jnp.stack(weights)
    own = lax.all_to_all(stacked, "core", split_axis=2, concat_axis=1, tiled=True)
    own = lax.all_gather(own, CHIPS, axis=1, tiled=True)
    other = swap_cores(own)
    return [(own[i], other[i]) for i in range(len(weights))]


def scatter_grads(*parts):
    pair_sums = []
    for own, other in parts:
        arrived = swap_cores(other.astype(jnp.bfloat16))
        pair_sums.append(
            (own.astype(jnp.bfloat16).astype(jnp.float32) + arrived.astype(jnp.float32)).astype(
                jnp.bfloat16
            )
        )
    chip_sum = lax.psum_scatter(jnp.stack(pair_sums), CHIPS, scatter_dimension=1, tiled=True)
    first = lax.axis_index("core") == 0
    rows = chip_sum.shape[1] // 2

    def my_rows(value):
        return jnp.where(first, value[:, :rows], value[:, rows:]).astype(jnp.float32)

    mine = my_rows(chip_sum)
    theirs = my_rows(swap_cores(chip_sum))
    block = jnp.where(
        first, jnp.concatenate([mine, theirs], axis=2), jnp.concatenate([theirs, mine], axis=2)
    )
    return [block[i] for i in range(len(parts))]


def halves(left, pair, dims):
    return (
        lax.dot_general(left, pair[0], dims, preferred_element_type=jnp.float32),
        lax.dot_general(left, pair[1], dims, preferred_element_type=jnp.float32),
    )


def shards(tokens, routes, gate_levels, w_gate, w_up, w_down, grad_out):
    experts = lax.axis_size("expert")
    tok_rows = tokens.shape[0]
    model_width = tokens.shape[1]
    capacity = min(tok_rows, tok_rows * TOP * 5 // (4 * experts))
    slot_count = experts * capacity
    expert_of = routes[:, 0]
    onehot = (expert_of[:, None] == jnp.arange(experts, dtype=jnp.int32)[None, :]).astype(jnp.int32)
    earlier = jnp.cumsum(onehot, axis=0) - onehot
    slot_rank = jnp.sum(earlier * onehot, axis=1)
    slot_index = expert_of * capacity + slot_rank
    source_row = (
        jnp.zeros((slot_count,), jnp.int32)
        .at[slot_index]
        .set(jnp.arange(tok_rows, dtype=jnp.int32))
    )
    filled = (
        jnp.zeros((slot_count, 1), jnp.bfloat16)
        .at[slot_index, 0]
        .set(jnp.ones((tok_rows,), jnp.bfloat16))
    )
    gate_weight = gate_levels.astype(jnp.float32) / 64.0

    def pack_rows(values):
        return (jnp.take(values, source_row, axis=0) * filled).reshape(
            experts, capacity, model_width
        )

    gate_pair, up_pair, down_pair = gather_weights(w_gate[0], w_up[0], w_down[0])
    plain = (((1,), (0,)), ((), ()))
    last = (((1,), (1,)), ((), ()))
    received = lax.all_to_all(
        pack_rows(tokens), "expert", split_axis=0, concat_axis=0, tiled=True
    ).reshape(slot_count, model_width)
    act_gate = jnp.concatenate(halves(received, gate_pair, plain), axis=1)
    act_up = jnp.concatenate(halves(received, up_pair, plain), axis=1)
    sigmoid_gate = jax.nn.sigmoid(act_gate)
    silu_gate = act_gate * sigmoid_gate
    hidden = (silu_gate * act_up).astype(jnp.bfloat16)
    half = hidden.shape[1] // 2
    expert_out = (
        (
            contract_last(hidden[:, :half], down_pair[0])
            + contract_last(hidden[:, half:], down_pair[1])
        )
        .astype(jnp.bfloat16)
        .reshape(experts, capacity, model_width)
    )
    returned = lax.all_to_all(
        expert_out, "expert", split_axis=0, concat_axis=0, tiled=True
    ).reshape(slot_count, model_width)
    moe_out = (gate_weight * jnp.take(returned, slot_index, axis=0).astype(jnp.float32)).astype(
        jnp.bfloat16
    )
    out_grad = (gate_weight * grad_out.astype(jnp.float32)).astype(jnp.bfloat16)
    grad_rows = lax.all_to_all(
        pack_rows(out_grad), "expert", split_axis=0, concat_axis=0, tiled=True
    ).reshape(slot_count, model_width)
    hidden_grad = jnp.concatenate(halves(grad_rows, down_pair, plain), axis=1)
    gate_delta = (
        hidden_grad * act_up * sigmoid_gate * (1.0 + act_gate * (1.0 - sigmoid_gate))
    ).astype(jnp.bfloat16)
    up_delta = (hidden_grad * silu_gate).astype(jnp.bfloat16)
    token_grad = (
        contract_last(gate_delta[:, :half], gate_pair[0])
        + contract_last(gate_delta[:, half:], gate_pair[1])
        + contract_last(up_delta[:, :half], up_pair[0])
        + contract_last(up_delta[:, half:], up_pair[1])
    ).astype(jnp.bfloat16)
    arrived = lax.all_to_all(
        token_grad.reshape(experts, capacity, model_width),
        "expert",
        split_axis=0,
        concat_axis=0,
        tiled=True,
    )
    grad_tokens = jnp.take(arrived.reshape(slot_count, model_width), slot_index, axis=0)
    grad_gate, grad_up, grad_down = scatter_grads(
        (contract_first(received, gate_delta[:, :half]), contract_first(received, gate_delta[:, half:])),
        (contract_first(received, up_delta[:, :half]), contract_first(received, up_delta[:, half:])),
        (contract_first(grad_rows, hidden[:, :half]), contract_first(grad_rows, hidden[:, half:])),
    )
    return (moe_out, grad_tokens, grad_gate[None], grad_up[None], grad_down[None])


def solution(mesh):
    dp_size, expert_size = mesh.devices.shape
    chips = dp_size // 2
    x_size = 4 if chips % 4 == 0 else 1
    grid = mesh.devices.reshape(x_size, chips // x_size, 2, expert_size)
    fine = Mesh(grid, DP + ("expert",))
    rows = P(DP + ("expert",), None)
    weights = P("expert", DP, None)
    in_specs = (rows, rows, rows, weights, weights, weights, rows)
    out_specs = (rows, rows, weights, weights, weights)
    return jax.shard_map(shards, mesh=fine, in_specs=in_specs, out_specs=out_specs, check_vma=False)
```

```python
import jax
import jax.numpy as jnp
from jax import lax
from jax.sharding import Mesh
from jax.sharding import PartitionSpec as P

TOP = 1
CHIPS = ("x", "zh")
DP = ("x", "zh", "core")


def contract_last(matrix_a, matrix_b):
    return lax.dot_general(
        matrix_a, matrix_b, (((1,), (1,)), ((), ())), preferred_element_type=jnp.float32
    )


def contract_first(matrix_a, matrix_b):
    return lax.dot_general(
        matrix_a, matrix_b, (((0,), (0,)), ((), ())), preferred_element_type=jnp.float32
    )


def swap_cores(value):
    return lax.ppermute(value, "core", perm=[(0, 1), (1, 0)])


def gather_weights(*weights):
    stacked = jnp.stack(weights)
    half = stacked.shape[2] // 2
    first = lax.axis_index("core") == 0
    kept = jnp.where(first, stacked[:, :, :half], stacked[:, :, half:])
    sent = jnp.where(first, stacked[:, :, half:], stacked[:, :, :half])
    came = swap_cores(sent)
    own = jnp.where(
        first, jnp.concatenate([kept, came], axis=1), jnp.concatenate([came, kept], axis=1)
    )
    own = lax.all_gather(own, CHIPS, axis=1, tiled=True)
    other = swap_cores(own)
    return [(own[i], other[i]) for i in range(len(weights))]


def scatter_grads(*parts):
    pair_sums = []
    for own, other in parts:
        arrived = swap_cores(other.astype(jnp.bfloat16))
        pair_sums.append(
            (own.astype(jnp.bfloat16).astype(jnp.float32) + arrived.astype(jnp.float32)).astype(
                jnp.bfloat16
            )
        )
    chip_sum = lax.psum_scatter(jnp.stack(pair_sums), CHIPS, scatter_dimension=1, tiled=True)
    first = lax.axis_index("core") == 0
    rows = chip_sum.shape[1] // 2

    def my_rows(value):
        return jnp.where(first, value[:, :rows], value[:, rows:]).astype(jnp.float32)

    mine = my_rows(chip_sum)
    theirs = my_rows(swap_cores(chip_sum))
    block = jnp.where(
        first, jnp.concatenate([mine, theirs], axis=2), jnp.concatenate([theirs, mine], axis=2)
    )
    return [block[i] for i in range(len(parts))]


def halves(left, pair, dims):
    return (
        lax.dot_general(left, pair[0], dims, preferred_element_type=jnp.float32),
        lax.dot_general(left, pair[1], dims, preferred_element_type=jnp.float32),
    )


def shards(tokens, routes, gate_levels, w_gate, w_up, w_down, grad_out):
    experts = lax.axis_size("expert")
    tok_rows = tokens.shape[0]
    model_width = tokens.shape[1]
    capacity = min(tok_rows, tok_rows * TOP * 5 // (4 * experts))
    slot_count = experts * capacity
    expert_of = routes[:, 0]
    onehot = (expert_of[:, None] == jnp.arange(experts, dtype=jnp.int32)[None, :]).astype(jnp.int32)
    earlier = jnp.cumsum(onehot, axis=0) - onehot
    slot_rank = jnp.sum(earlier * onehot, axis=1)
    slot_index = expert_of * capacity + slot_rank
    source_row = (
        jnp.zeros((slot_count,), jnp.int32)
        .at[slot_index]
        .set(jnp.arange(tok_rows, dtype=jnp.int32))
    )
    filled = (
        jnp.zeros((slot_count, 1), jnp.bfloat16)
        .at[slot_index, 0]
        .set(jnp.ones((tok_rows,), jnp.bfloat16))
    )
    gate_weight = gate_levels.astype(jnp.float32) / 64.0

    def pack_rows(values):
        return (jnp.take(values, source_row, axis=0) * filled).reshape(
            experts, capacity, model_width
        )

    gate_pair, up_pair, down_pair = gather_weights(w_gate[0], w_up[0], w_down[0])
    plain = (((1,), (0,)), ((), ()))
    last = (((1,), (1,)), ((), ()))
    out_grad = (gate_weight * grad_out.astype(jnp.float32)).astype(jnp.bfloat16)
    both_rows = lax.all_to_all(
        jnp.stack([pack_rows(tokens), pack_rows(out_grad)]),
        "expert",
        split_axis=1,
        concat_axis=1,
        tiled=True,
    )
    received = both_rows[0].reshape(slot_count, model_width)
    grad_rows = both_rows[1].reshape(slot_count, model_width)
    act_gate = jnp.concatenate(halves(received, gate_pair, plain), axis=1)
    act_up = jnp.concatenate(halves(received, up_pair, plain), axis=1)
    sigmoid_gate = jax.nn.sigmoid(act_gate)
    silu_gate = act_gate * sigmoid_gate
    hidden = (silu_gate * act_up).astype(jnp.bfloat16)
    half = hidden.shape[1] // 2
    expert_out = (
        (
            contract_last(hidden[:, :half], down_pair[0])
            + contract_last(hidden[:, half:], down_pair[1])
        )
        .astype(jnp.bfloat16)
        .reshape(experts, capacity, model_width)
    )
    returned = lax.all_to_all(
        expert_out, "expert", split_axis=0, concat_axis=0, tiled=True
    ).reshape(slot_count, model_width)
    moe_out = (gate_weight * jnp.take(returned, slot_index, axis=0).astype(jnp.float32)).astype(
        jnp.bfloat16
    )
    hidden_grad = jnp.concatenate(halves(grad_rows, down_pair, plain), axis=1)
    gate_delta = (
        hidden_grad * act_up * sigmoid_gate * (1.0 + act_gate * (1.0 - sigmoid_gate))
    ).astype(jnp.bfloat16)
    up_delta = (hidden_grad * silu_gate).astype(jnp.bfloat16)
    token_grad = (
        contract_last(gate_delta[:, :half], gate_pair[0])
        + contract_last(gate_delta[:, half:], gate_pair[1])
        + contract_last(up_delta[:, :half], up_pair[0])
        + contract_last(up_delta[:, half:], up_pair[1])
    ).astype(jnp.bfloat16)
    arrived = lax.all_to_all(
        token_grad.reshape(experts, capacity, model_width),
        "expert",
        split_axis=0,
        concat_axis=0,
        tiled=True,
    )
    grad_tokens = jnp.take(arrived.reshape(slot_count, model_width), slot_index, axis=0)
    grad_gate, grad_up, grad_down = scatter_grads(
        (contract_first(received, gate_delta[:, :half]), contract_first(received, gate_delta[:, half:])),
        (contract_first(received, up_delta[:, :half]), contract_first(received, up_delta[:, half:])),
        (contract_first(grad_rows, hidden[:, :half]), contract_first(grad_rows, hidden[:, half:])),
    )
    return (moe_out, grad_tokens, grad_gate[None], grad_up[None], grad_down[None])


def solution(mesh):
    dp_size, expert_size = mesh.devices.shape
    chips = dp_size // 2
    x_size = 4 if chips % 4 == 0 else 1
    grid = mesh.devices.reshape(x_size, chips // x_size, 2, expert_size)
    fine = Mesh(grid, DP + ("expert",))
    rows = P(DP + ("expert",), None)
    weights = P("expert", DP, None)
    in_specs = (rows, rows, rows, weights, weights, weights, rows)
    out_specs = (rows, rows, weights, weights, weights)
    return jax.shard_map(shards, mesh=fine, in_specs=in_specs, out_specs=out_specs, check_vma=False)
```

```python
import jax
import jax.numpy as jnp
from jax import lax
from jax.sharding import Mesh
from jax.sharding import PartitionSpec as P

TOP = 1
CHIPS = ("x", "zh")
DP = ("x", "zh", "core")


def contract_last(matrix_a, matrix_b):
    return lax.dot_general(
        matrix_a, matrix_b, (((1,), (1,)), ((), ())), preferred_element_type=jnp.float32
    )


def contract_first(matrix_a, matrix_b):
    return lax.dot_general(
        matrix_a, matrix_b, (((0,), (0,)), ((), ())), preferred_element_type=jnp.float32
    )


def swap_cores(value):
    return lax.ppermute(value, "core", perm=[(0, 1), (1, 0)])


def gather_weights(*weights):
    stacked = jnp.stack(weights)
    half = stacked.shape[2] // 2
    first = lax.axis_index("core") == 0
    kept = jnp.where(first, stacked[:, :, :half], stacked[:, :, half:])
    sent = jnp.where(first, stacked[:, :, half:], stacked[:, :, :half])
    came = swap_cores(sent)
    own = jnp.where(
        first, jnp.concatenate([kept, came], axis=1), jnp.concatenate([came, kept], axis=1)
    )
    gathered = lax.all_gather(own[:-1], CHIPS, axis=1, tiled=True)
    last = ring_gather(own[-1])
    owns = [gathered[i] for i in range(len(weights) - 1)] + [last]
    return [(value, swap_cores(value)) for value in owns]


def ring_stage(value, axis):
    size = lax.axis_size(axis)
    me = lax.axis_index(axis)
    held = jnp.zeros((size,) + value.shape, value.dtype)
    held = lax.dynamic_update_index_in_dim(held, value, me, 0)
    for shift in range(1, size):
        got = lax.ppermute(value, axis, perm=[(i, (i + shift) % size) for i in range(size)])
        held = lax.dynamic_update_index_in_dim(held, got, (me - shift) % size, 0)
    return held


def ring_gather(block):
    by_zh = ring_stage(block, CHIPS[1])
    by_x = ring_stage(by_zh, CHIPS[0])
    return by_x.reshape((-1,) + block.shape[1:])


def scatter_grads(*parts):
    pair_sums = []
    for own, other in parts:
        arrived = swap_cores(other.astype(jnp.bfloat16))
        pair_sums.append(
            (own.astype(jnp.bfloat16).astype(jnp.float32) + arrived.astype(jnp.float32)).astype(
                jnp.bfloat16
            )
        )
    chip_sum = lax.psum_scatter(jnp.stack(pair_sums), CHIPS, scatter_dimension=1, tiled=True)
    first = lax.axis_index("core") == 0
    rows = chip_sum.shape[1] // 2

    def my_rows(value):
        return jnp.where(first, value[:, :rows], value[:, rows:]).astype(jnp.float32)

    mine = my_rows(chip_sum)
    theirs = my_rows(swap_cores(chip_sum))
    block = jnp.where(
        first, jnp.concatenate([mine, theirs], axis=2), jnp.concatenate([theirs, mine], axis=2)
    )
    return [block[i] for i in range(len(parts))]


def halves(left, pair, dims):
    return (
        lax.dot_general(left, pair[0], dims, preferred_element_type=jnp.float32),
        lax.dot_general(left, pair[1], dims, preferred_element_type=jnp.float32),
    )


def shards(tokens, routes, gate_levels, w_gate, w_up, w_down, grad_out):
    experts = lax.axis_size("expert")
    tok_rows = tokens.shape[0]
    model_width = tokens.shape[1]
    capacity = min(tok_rows, tok_rows * TOP * 5 // (4 * experts))
    slot_count = experts * capacity
    expert_of = routes[:, 0]
    onehot = (expert_of[:, None] == jnp.arange(experts, dtype=jnp.int32)[None, :]).astype(jnp.int32)
    earlier = jnp.cumsum(onehot, axis=0) - onehot
    slot_rank = jnp.sum(earlier * onehot, axis=1)
    slot_index = expert_of * capacity + slot_rank
    source_row = (
        jnp.zeros((slot_count,), jnp.int32)
        .at[slot_index]
        .set(jnp.arange(tok_rows, dtype=jnp.int32))
    )
    filled = (
        jnp.zeros((slot_count, 1), jnp.bfloat16)
        .at[slot_index, 0]
        .set(jnp.ones((tok_rows,), jnp.bfloat16))
    )
    gate_weight = gate_levels.astype(jnp.float32) / 64.0

    def pack_rows(values):
        return (jnp.take(values, source_row, axis=0) * filled).reshape(
            experts, capacity, model_width
        )

    gate_pair, up_pair, down_pair = gather_weights(w_gate[0], w_up[0], w_down[0])
    plain = (((1,), (0,)), ((), ()))
    last = (((1,), (1,)), ((), ()))
    out_grad = (gate_weight * grad_out.astype(jnp.float32)).astype(jnp.bfloat16)
    both_rows = lax.all_to_all(
        jnp.stack([pack_rows(tokens), pack_rows(out_grad)]),
        "expert",
        split_axis=1,
        concat_axis=1,
        tiled=True,
    )
    received = both_rows[0].reshape(slot_count, model_width)
    grad_rows = both_rows[1].reshape(slot_count, model_width)
    act_gate = jnp.concatenate(halves(received, gate_pair, plain), axis=1)
    act_up = jnp.concatenate(halves(received, up_pair, plain), axis=1)
    sigmoid_gate = jax.nn.sigmoid(act_gate)
    silu_gate = act_gate * sigmoid_gate
    hidden = (silu_gate * act_up).astype(jnp.bfloat16)
    half = hidden.shape[1] // 2
    expert_out = (
        (
            contract_last(hidden[:, :half], down_pair[0])
            + contract_last(hidden[:, half:], down_pair[1])
        )
        .astype(jnp.bfloat16)
        .reshape(experts, capacity, model_width)
    )
    returned = lax.all_to_all(
        expert_out, "expert", split_axis=0, concat_axis=0, tiled=True
    ).reshape(slot_count, model_width)
    moe_out = (gate_weight * jnp.take(returned, slot_index, axis=0).astype(jnp.float32)).astype(
        jnp.bfloat16
    )
    hidden_grad = jnp.concatenate(halves(grad_rows, down_pair, plain), axis=1)
    gate_delta = (
        hidden_grad * act_up * sigmoid_gate * (1.0 + act_gate * (1.0 - sigmoid_gate))
    ).astype(jnp.bfloat16)
    up_delta = (hidden_grad * silu_gate).astype(jnp.bfloat16)
    token_grad = (
        contract_last(gate_delta[:, :half], gate_pair[0])
        + contract_last(gate_delta[:, half:], gate_pair[1])
        + contract_last(up_delta[:, :half], up_pair[0])
        + contract_last(up_delta[:, half:], up_pair[1])
    ).astype(jnp.bfloat16)
    arrived = lax.all_to_all(
        token_grad.reshape(experts, capacity, model_width),
        "expert",
        split_axis=0,
        concat_axis=0,
        tiled=True,
    )
    grad_tokens = jnp.take(arrived.reshape(slot_count, model_width), slot_index, axis=0)
    grad_gate, grad_up, grad_down = scatter_grads(
        (contract_first(received, gate_delta[:, :half]), contract_first(received, gate_delta[:, half:])),
        (contract_first(received, up_delta[:, :half]), contract_first(received, up_delta[:, half:])),
        (contract_first(grad_rows, hidden[:, :half]), contract_first(grad_rows, hidden[:, half:])),
    )
    return (moe_out, grad_tokens, grad_gate[None], grad_up[None], grad_down[None])


def solution(mesh):
    dp_size, expert_size = mesh.devices.shape
    chips = dp_size // 2
    x_size = 4 if chips % 4 == 0 else 1
    grid = mesh.devices.reshape(x_size, chips // x_size, 2, expert_size)
    fine = Mesh(grid, DP + ("expert",))
    rows = P(DP + ("expert",), None)
    weights = P("expert", DP, None)
    in_specs = (rows, rows, rows, weights, weights, weights, rows)
    out_specs = (rows, rows, weights, weights, weights)
    return jax.shard_map(shards, mesh=fine, in_specs=in_specs, out_specs=out_specs, check_vma=False)
```

```python
import jax
import jax.numpy as jnp
from jax import lax
from jax.sharding import Mesh
from jax.sharding import PartitionSpec as P

TOP = 1
CHIPS = ("x", "zh")
DP = ("x", "zh", "core")


def contract_last(matrix_a, matrix_b):
    return lax.dot_general(
        matrix_a, matrix_b, (((1,), (1,)), ((), ())), preferred_element_type=jnp.float32
    )


def contract_first(matrix_a, matrix_b):
    return lax.dot_general(
        matrix_a, matrix_b, (((0,), (0,)), ((), ())), preferred_element_type=jnp.float32
    )


def swap_cores(value):
    return lax.ppermute(value, "core", perm=[(0, 1), (1, 0)])


def gather_weights(*weights):
    stacked = jnp.stack(weights)
    half = stacked.shape[2] // 2
    first = lax.axis_index("core") == 0
    kept = jnp.where(first, stacked[:, :, :half], stacked[:, :, half:])
    sent = jnp.where(first, stacked[:, :, half:], stacked[:, :, :half])
    came = swap_cores(sent)
    own = jnp.where(
        first, jnp.concatenate([kept, came], axis=1), jnp.concatenate([came, kept], axis=1)
    )
    own = lax.all_gather(own, CHIPS, axis=1, tiled=True)
    return [(own[i], swap_cores(own[i])) for i in range(len(weights))]


def scatter_grads(*parts):
    pair_sums = []
    for own, other in parts:
        arrived = swap_cores(other.astype(jnp.bfloat16))
        pair_sums.append(
            (own.astype(jnp.bfloat16).astype(jnp.float32) + arrived.astype(jnp.float32)).astype(
                jnp.bfloat16
            )
        )
    chip_sum = lax.psum_scatter(jnp.stack(pair_sums), CHIPS, scatter_dimension=1, tiled=True)
    first = lax.axis_index("core") == 0
    rows = chip_sum.shape[1] // 2

    def my_rows(value):
        return jnp.where(first, value[:, :rows], value[:, rows:]).astype(jnp.float32)

    mine = my_rows(chip_sum)
    theirs = my_rows(swap_cores(chip_sum))
    block = jnp.where(
        first, jnp.concatenate([mine, theirs], axis=2), jnp.concatenate([theirs, mine], axis=2)
    )
    return [block[i] for i in range(len(parts))]


def halves(left, pair, dims):
    return (
        lax.dot_general(left, pair[0], dims, preferred_element_type=jnp.float32),
        lax.dot_general(left, pair[1], dims, preferred_element_type=jnp.float32),
    )


def shards(tokens, routes, gate_levels, w_gate, w_up, w_down, grad_out):
    experts = lax.axis_size("expert")
    tok_rows = tokens.shape[0]
    model_width = tokens.shape[1]
    capacity = min(tok_rows, tok_rows * TOP * 5 // (4 * experts))
    slot_count = experts * capacity
    expert_of = routes[:, 0]
    onehot = (expert_of[:, None] == jnp.arange(experts, dtype=jnp.int32)[None, :]).astype(jnp.int32)
    earlier = jnp.cumsum(onehot, axis=0) - onehot
    slot_rank = jnp.sum(earlier * onehot, axis=1)
    slot_index = expert_of * capacity + slot_rank
    source_row = (
        jnp.zeros((slot_count,), jnp.int32)
        .at[slot_index]
        .set(jnp.arange(tok_rows, dtype=jnp.int32))
    )
    filled = (
        jnp.zeros((slot_count, 1), jnp.bfloat16)
        .at[slot_index, 0]
        .set(jnp.ones((tok_rows,), jnp.bfloat16))
    )
    gate_weight = gate_levels.astype(jnp.float32) / 64.0

    def pack_rows(values):
        return (jnp.take(values, source_row, axis=0) * filled).reshape(
            experts, capacity, model_width
        )

    gate_pair, up_pair, down_pair = gather_weights(w_gate[0], w_up[0], w_down[0])
    plain = (((1,), (0,)), ((), ()))
    last = (((1,), (1,)), ((), ()))
    out_grad = (gate_weight * grad_out.astype(jnp.float32)).astype(jnp.bfloat16)
    both_rows = lax.all_to_all(
        jnp.stack([pack_rows(tokens), pack_rows(out_grad)]),
        "expert",
        split_axis=1,
        concat_axis=1,
        tiled=True,
    )
    received = both_rows[0].reshape(slot_count, model_width)
    grad_rows = both_rows[1].reshape(slot_count, model_width)
    act_gate = jnp.concatenate(halves(received, gate_pair, plain), axis=1)
    act_up = jnp.concatenate(halves(received, up_pair, plain), axis=1)
    sigmoid_gate = jax.nn.sigmoid(act_gate)
    silu_gate = act_gate * sigmoid_gate
    hidden = (silu_gate * act_up).astype(jnp.bfloat16)
    half = hidden.shape[1] // 2
    expert_out = (
        (
            contract_last(hidden[:, :half], down_pair[0])
            + contract_last(hidden[:, half:], down_pair[1])
        )
        .astype(jnp.bfloat16)
        .reshape(experts, capacity, model_width)
    )
    returned = lax.all_to_all(
        expert_out, "expert", split_axis=0, concat_axis=0, tiled=True
    ).reshape(slot_count, model_width)
    moe_out = (gate_weight * jnp.take(returned, slot_index, axis=0).astype(jnp.float32)).astype(
        jnp.bfloat16
    )
    hidden_grad = jnp.concatenate(halves(grad_rows, down_pair, plain), axis=1)
    gate_delta = (
        hidden_grad * act_up * sigmoid_gate * (1.0 + act_gate * (1.0 - sigmoid_gate))
    ).astype(jnp.bfloat16)
    up_delta = (hidden_grad * silu_gate).astype(jnp.bfloat16)
    token_grad = (
        contract_last(gate_delta[:, :half], gate_pair[0])
        + contract_last(gate_delta[:, half:], gate_pair[1])
        + contract_last(up_delta[:, :half], up_pair[0])
        + contract_last(up_delta[:, half:], up_pair[1])
    ).astype(jnp.bfloat16)
    arrived = lax.all_to_all(
        token_grad.reshape(experts, capacity, model_width),
        "expert",
        split_axis=0,
        concat_axis=0,
        tiled=True,
    )
    grad_tokens = jnp.take(arrived.reshape(slot_count, model_width), slot_index, axis=0)
    grad_gate, grad_up, grad_down = scatter_grads(
        (contract_first(received, gate_delta[:, :half]), contract_first(received, gate_delta[:, half:])),
        (contract_first(received, up_delta[:, :half]), contract_first(received, up_delta[:, half:])),
        (contract_first(grad_rows, hidden[:, :half]), contract_first(grad_rows, hidden[:, half:])),
    )
    return (moe_out, grad_tokens, grad_gate[None], grad_up[None], grad_down[None])


def solution(mesh):
    dp_size, expert_size = mesh.devices.shape
    chips = dp_size // 2
    x_size = 4 if chips % 4 == 0 else 1
    grid = mesh.devices.reshape(x_size, chips // x_size, 2, expert_size)
    fine = Mesh(grid, DP + ("expert",))
    rows = P(DP + ("expert",), None)
    weights = P("expert", DP, None)
    in_specs = (rows, rows, rows, weights, weights, weights, rows)
    out_specs = (rows, rows, weights, weights, weights)
    return jax.shard_map(shards, mesh=fine, in_specs=in_specs, out_specs=out_specs, check_vma=False)
```

```python
import jax
import jax.numpy as jnp
from jax import lax
from jax.sharding import Mesh
from jax.sharding import PartitionSpec as P

TOP = 1
CHIPS = ("x", "zh")
DP = ("x", "zh", "core")


def contract_last(matrix_a, matrix_b):
    return lax.dot_general(
        matrix_a, matrix_b, (((1,), (1,)), ((), ())), preferred_element_type=jnp.float32
    )


def contract_first(matrix_a, matrix_b):
    return lax.dot_general(
        matrix_a, matrix_b, (((0,), (0,)), ((), ())), preferred_element_type=jnp.float32
    )


def swap_cores(value):
    return lax.ppermute(value, "core", perm=[(0, 1), (1, 0)])


def gather_weights(*weights):
    stacked = jnp.stack(weights)
    half = stacked.shape[2] // 2
    first = lax.axis_index("core") == 0
    kept = jnp.where(first, stacked[:, :, :half], stacked[:, :, half:])
    sent = jnp.where(first, stacked[:, :, half:], stacked[:, :, :half])
    came = swap_cores(sent)
    own = jnp.where(
        first, jnp.concatenate([kept, came], axis=1), jnp.concatenate([came, kept], axis=1)
    )
    own = lax.all_gather(own, CHIPS, axis=1, tiled=True)
    other = swap_cores(own)
    return [(own[i], other[i]) for i in range(len(weights))]


def scatter_grads(lefts, rights):
    half = rights.shape[2] // 2
    batched = (((1,), (1,)), ((0,), (0,)))
    other = lax.dot_general(lefts, rights[:, :, half:], batched, preferred_element_type=jnp.float32)
    arrived = swap_cores(other.astype(jnp.bfloat16))
    own = lax.dot_general(lefts, rights[:, :, :half], batched, preferred_element_type=jnp.float32)
    pair_sum = (own.astype(jnp.bfloat16).astype(jnp.float32) + arrived.astype(jnp.float32)).astype(
        jnp.bfloat16
    )
    chip_sum = lax.psum_scatter(pair_sum, CHIPS, scatter_dimension=1, tiled=True)
    first = lax.axis_index("core") == 0
    rows = chip_sum.shape[1] // 2

    def my_rows(value):
        return jnp.where(first, value[:, :rows], value[:, rows:]).astype(jnp.float32)

    mine = my_rows(chip_sum)
    theirs = my_rows(swap_cores(chip_sum))
    block = jnp.where(
        first, jnp.concatenate([mine, theirs], axis=2), jnp.concatenate([theirs, mine], axis=2)
    )
    return [block[i] for i in range(block.shape[0])]


def halves(left, pair, dims):
    return (
        lax.dot_general(left, pair[0], dims, preferred_element_type=jnp.float32),
        lax.dot_general(left, pair[1], dims, preferred_element_type=jnp.float32),
    )


def shards(tokens, routes, gate_levels, w_gate, w_up, w_down, grad_out):
    experts = lax.axis_size("expert")
    tok_rows = tokens.shape[0]
    model_width = tokens.shape[1]
    capacity = min(tok_rows, tok_rows * TOP * 5 // (4 * experts))
    slot_count = experts * capacity
    expert_of = routes[:, 0]
    onehot = (expert_of[:, None] == jnp.arange(experts, dtype=jnp.int32)[None, :]).astype(jnp.int32)
    earlier = jnp.cumsum(onehot, axis=0) - onehot
    slot_rank = jnp.sum(earlier * onehot, axis=1)
    slot_index = expert_of * capacity + slot_rank
    source_row = (
        jnp.zeros((slot_count,), jnp.int32)
        .at[slot_index]
        .set(jnp.arange(tok_rows, dtype=jnp.int32))
    )
    filled = (
        jnp.zeros((slot_count, 1), jnp.bfloat16)
        .at[slot_index, 0]
        .set(jnp.ones((tok_rows,), jnp.bfloat16))
    )
    gate_weight = gate_levels.astype(jnp.float32) / 64.0

    def pack_rows(values):
        return (jnp.take(values, source_row, axis=0) * filled).reshape(
            experts, capacity, model_width
        )

    gate_pair, up_pair, down_pair = gather_weights(w_gate[0], w_up[0], w_down[0])
    plain = (((1,), (0,)), ((), ()))
    last = (((1,), (1,)), ((), ()))
    out_grad = (gate_weight * grad_out.astype(jnp.float32)).astype(jnp.bfloat16)
    both_rows = lax.all_to_all(
        jnp.stack([pack_rows(tokens), pack_rows(out_grad)]),
        "expert",
        split_axis=1,
        concat_axis=1,
        tiled=True,
    )
    received = both_rows[0].reshape(slot_count, model_width)
    grad_rows = both_rows[1].reshape(slot_count, model_width)
    act_gate = jnp.concatenate(halves(received, gate_pair, plain), axis=1)
    act_up = jnp.concatenate(halves(received, up_pair, plain), axis=1)
    sigmoid_gate = jax.nn.sigmoid(act_gate)
    silu_gate = act_gate * sigmoid_gate
    hidden = (silu_gate * act_up).astype(jnp.bfloat16)
    half = hidden.shape[1] // 2
    expert_out = (
        (
            contract_last(hidden[:, :half], down_pair[0])
            + contract_last(hidden[:, half:], down_pair[1])
        )
        .astype(jnp.bfloat16)
        .reshape(experts, capacity, model_width)
    )
    returned = lax.all_to_all(
        expert_out, "expert", split_axis=0, concat_axis=0, tiled=True
    ).reshape(slot_count, model_width)
    moe_out = (gate_weight * jnp.take(returned, slot_index, axis=0).astype(jnp.float32)).astype(
        jnp.bfloat16
    )
    hidden_grad = jnp.concatenate(halves(grad_rows, down_pair, plain), axis=1)
    gate_delta = (
        hidden_grad * act_up * sigmoid_gate * (1.0 + act_gate * (1.0 - sigmoid_gate))
    ).astype(jnp.bfloat16)
    up_delta = (hidden_grad * silu_gate).astype(jnp.bfloat16)
    token_grad = (
        contract_last(gate_delta[:, :half], gate_pair[0])
        + contract_last(gate_delta[:, half:], gate_pair[1])
        + contract_last(up_delta[:, :half], up_pair[0])
        + contract_last(up_delta[:, half:], up_pair[1])
    ).astype(jnp.bfloat16)
    arrived = lax.all_to_all(
        token_grad.reshape(experts, capacity, model_width),
        "expert",
        split_axis=0,
        concat_axis=0,
        tiled=True,
    )
    grad_tokens = jnp.take(arrived.reshape(slot_count, model_width), slot_index, axis=0)
    grad_gate, grad_up, grad_down = scatter_grads(
        jnp.stack([received, received, grad_rows]), jnp.stack([gate_delta, up_delta, hidden])
    )
    return (moe_out, grad_tokens, grad_gate[None], grad_up[None], grad_down[None])


def solution(mesh):
    dp_size, expert_size = mesh.devices.shape
    chips = dp_size // 2
    x_size = 4 if chips % 4 == 0 else 1
    grid = mesh.devices.reshape(x_size, chips // x_size, 2, expert_size)
    fine = Mesh(grid, DP + ("expert",))
    rows = P(DP + ("expert",), None)
    weights = P("expert", DP, None)
    in_specs = (rows, rows, rows, weights, weights, weights, rows)
    out_specs = (rows, rows, weights, weights, weights)
    return jax.shard_map(shards, mesh=fine, in_specs=in_specs, out_specs=out_specs, check_vma=False)
```

```python
import jax
import jax.numpy as jnp
from jax import lax
from jax.sharding import Mesh
from jax.sharding import PartitionSpec as P

TOP = 1
CHIPS = ("x", "zh")
DP = ("x", "zh", "core")


def contract_last(matrix_a, matrix_b):
    return lax.dot_general(
        matrix_a, matrix_b, (((1,), (1,)), ((), ())), preferred_element_type=jnp.float32
    )


def contract_first(matrix_a, matrix_b):
    return lax.dot_general(
        matrix_a, matrix_b, (((0,), (0,)), ((), ())), preferred_element_type=jnp.float32
    )


def swap_cores(value):
    return lax.ppermute(value, "core", perm=[(0, 1), (1, 0)])


def gather_weights(*weights):
    half = weights[0].shape[1] // 2
    first = lax.axis_index("core") == 0
    kept = jnp.stack([jnp.where(first, w[:, :half], w[:, half:]) for w in weights])
    sent = jnp.stack([jnp.where(first, w[:, half:], w[:, :half]) for w in weights])
    came = swap_cores(sent)
    own = jnp.where(
        first, jnp.concatenate([kept, came], axis=1), jnp.concatenate([came, kept], axis=1)
    )
    own = lax.all_gather(own, CHIPS, axis=1, tiled=True)
    return [own[i] for i in range(len(weights))]


def scatter_grads(*parts):
    stacked = jnp.stack(parts).astype(jnp.bfloat16)
    chip_sum = lax.psum_scatter(stacked, CHIPS, scatter_dimension=1, tiled=True)
    first = lax.axis_index("core") == 0
    rows = chip_sum.shape[1] // 2

    def my_rows(value):
        return jnp.where(first, value[:, :rows], value[:, rows:]).astype(jnp.float32)

    mine = my_rows(chip_sum)
    theirs = my_rows(swap_cores(chip_sum))
    block = jnp.where(
        first, jnp.concatenate([mine, theirs], axis=2), jnp.concatenate([theirs, mine], axis=2)
    )
    return [block[i] for i in range(len(parts))]


def pair_total(partial, slots):
    arrived = swap_cores(partial[slots:])
    return (partial[:slots] + arrived).astype(jnp.bfloat16)


def shards(tokens, routes, gate_levels, w_gate, w_up, w_down, grad_out):
    experts = lax.axis_size("expert")
    tok_rows = tokens.shape[0]
    model_width = tokens.shape[1]
    capacity = min(tok_rows, tok_rows * TOP * 5 // (4 * experts))
    slot_count = experts * capacity
    expert_of = routes[:, 0]
    onehot = (expert_of[:, None] == jnp.arange(experts, dtype=jnp.int32)[None, :]).astype(jnp.int32)
    earlier = jnp.cumsum(onehot, axis=0) - onehot
    slot_rank = jnp.sum(earlier * onehot, axis=1)
    slot_index = expert_of * capacity + slot_rank
    source_row = (
        jnp.zeros((slot_count,), jnp.int32)
        .at[slot_index]
        .set(jnp.arange(tok_rows, dtype=jnp.int32))
    )
    filled = (
        jnp.zeros((slot_count, 1), jnp.bfloat16)
        .at[slot_index, 0]
        .set(jnp.ones((tok_rows,), jnp.bfloat16))
    )
    gate_weight = gate_levels.astype(jnp.float32) / 64.0

    def pack_rows(values):
        return (jnp.take(values, source_row, axis=0) * filled).reshape(
            experts, capacity, model_width
        )

    gate_own, up_own, down_own = gather_weights(w_gate[0], w_up[0], w_down[0])
    out_grad = (gate_weight * grad_out.astype(jnp.float32)).astype(jnp.bfloat16)
    both_rows = lax.all_to_all(
        jnp.stack([pack_rows(tokens), pack_rows(out_grad)]),
        "expert",
        split_axis=1,
        concat_axis=1,
        tiled=True,
    ).reshape(2, slot_count, model_width)
    pair_rows = jnp.concatenate([both_rows, swap_cores(both_rows)], axis=1)
    received = pair_rows[0]
    grad_rows = pair_rows[1]
    act_gate = jnp.dot(received, gate_own, preferred_element_type=jnp.float32)
    act_up = jnp.dot(received, up_own, preferred_element_type=jnp.float32)
    sigmoid_gate = jax.nn.sigmoid(act_gate)
    silu_gate = act_gate * sigmoid_gate
    hidden = (silu_gate * act_up).astype(jnp.bfloat16)
    hidden_grad = jnp.dot(grad_rows, down_own, preferred_element_type=jnp.float32)
    gate_delta = (
        hidden_grad * act_up * sigmoid_gate * (1.0 + act_gate * (1.0 - sigmoid_gate))
    ).astype(jnp.bfloat16)
    up_delta = (hidden_grad * silu_gate).astype(jnp.bfloat16)
    grad_gate, grad_up, grad_down = scatter_grads(
        contract_first(received, gate_delta),
        contract_first(received, up_delta),
        contract_first(grad_rows, hidden),
    )
    expert_out = pair_total(contract_last(hidden, down_own), slot_count).reshape(
        experts, capacity, model_width
    )
    returned = lax.all_to_all(
        expert_out, "expert", split_axis=0, concat_axis=0, tiled=True
    ).reshape(slot_count, model_width)
    moe_out = (gate_weight * jnp.take(returned, slot_index, axis=0).astype(jnp.float32)).astype(
        jnp.bfloat16
    )
    token_grad = pair_total(
        contract_last(gate_delta, gate_own) + contract_last(up_delta, up_own), slot_count
    )
    arrived = lax.all_to_all(
        token_grad.reshape(experts, capacity, model_width),
        "expert",
        split_axis=0,
        concat_axis=0,
        tiled=True,
    )
    grad_tokens = jnp.take(arrived.reshape(slot_count, model_width), slot_index, axis=0)
    return (moe_out, grad_tokens, grad_gate[None], grad_up[None], grad_down[None])


def solution(mesh):
    dp_size, expert_size = mesh.devices.shape
    chips = dp_size // 2
    x_size = 4 if chips % 4 == 0 else 1
    grid = mesh.devices.reshape(x_size, chips // x_size, 2, expert_size)
    fine = Mesh(grid, DP + ("expert",))
    rows = P(DP + ("expert",), None)
    weights = P("expert", DP, None)
    in_specs = (rows, rows, rows, weights, weights, weights, rows)
    out_specs = (rows, rows, weights, weights, weights)
    return jax.shard_map(shards, mesh=fine, in_specs=in_specs, out_specs=out_specs, check_vma=False)
```

```python
import jax
import jax.numpy as jnp
from jax import lax
from jax.sharding import Mesh
from jax.sharding import PartitionSpec as P

TOP = 1
CHIPS = ("x", "zh")
DP = ("x", "zh", "core")


def contract_last(matrix_a, matrix_b):
    return lax.dot_general(
        matrix_a, matrix_b, (((1,), (1,)), ((), ())), preferred_element_type=jnp.float32
    )


def contract_first(matrix_a, matrix_b):
    return lax.dot_general(
        matrix_a, matrix_b, (((0,), (0,)), ((), ())), preferred_element_type=jnp.float32
    )


def swap_cores(value):
    return lax.ppermute(value, "core", perm=[(0, 1), (1, 0)])


def gather_weights(*weights):
    half = weights[0].shape[1] // 2
    first = lax.axis_index("core") == 0
    kept = jnp.stack([jnp.where(first, w[:, :half], w[:, half:]) for w in weights])
    sent = jnp.stack([jnp.where(first, w[:, half:], w[:, :half]) for w in weights])
    came = swap_cores(sent)
    own = jnp.where(
        first, jnp.concatenate([kept, came], axis=1), jnp.concatenate([came, kept], axis=1)
    )
    own = lax.all_gather(own, CHIPS, axis=1, tiled=True)
    return [own[i] for i in range(len(weights))]


def scatter_grads(*parts):
    stacked = jnp.stack([part.astype(jnp.bfloat16) for part in parts])
    chip_sum = lax.psum_scatter(stacked, CHIPS, scatter_dimension=1, tiled=True)
    first = lax.axis_index("core") == 0
    rows = chip_sum.shape[1] // 2

    def my_rows(value):
        return jnp.where(first, value[:, :rows], value[:, rows:]).astype(jnp.float32)

    mine = my_rows(chip_sum)
    theirs = my_rows(swap_cores(chip_sum))
    block = jnp.where(
        first, jnp.concatenate([mine, theirs], axis=2), jnp.concatenate([theirs, mine], axis=2)
    )
    return [block[i] for i in range(len(parts))]


def pair_total(partial, slots):
    arrived = swap_cores(partial[slots:])
    return (partial[:slots] + arrived).astype(jnp.bfloat16)


def shards(tokens, routes, gate_levels, w_gate, w_up, w_down, grad_out):
    experts = lax.axis_size("expert")
    tok_rows = tokens.shape[0]
    model_width = tokens.shape[1]
    capacity = min(tok_rows, tok_rows * TOP * 5 // (4 * experts))
    slot_count = experts * capacity
    expert_of = routes[:, 0]
    onehot = (expert_of[:, None] == jnp.arange(experts, dtype=jnp.int32)[None, :]).astype(jnp.int32)
    earlier = jnp.cumsum(onehot, axis=0) - onehot
    slot_rank = jnp.sum(earlier * onehot, axis=1)
    slot_index = expert_of * capacity + slot_rank
    source_row = (
        jnp.zeros((slot_count,), jnp.int32)
        .at[slot_index]
        .set(jnp.arange(tok_rows, dtype=jnp.int32))
    )
    filled = (
        jnp.zeros((slot_count, 1), jnp.bfloat16)
        .at[slot_index, 0]
        .set(jnp.ones((tok_rows,), jnp.bfloat16))
    )
    gate_weight = gate_levels.astype(jnp.float32) / 64.0

    def pack_rows(values):
        return (jnp.take(values, source_row, axis=0) * filled).reshape(
            experts, capacity, model_width
        )

    gate_own, up_own, down_own = gather_weights(w_gate[0], w_up[0], w_down[0])
    out_grad = (gate_weight * grad_out.astype(jnp.float32)).astype(jnp.bfloat16)
    both_rows = lax.all_to_all(
        jnp.stack([pack_rows(tokens), pack_rows(out_grad)]),
        "expert",
        split_axis=1,
        concat_axis=1,
        tiled=True,
    ).reshape(2, slot_count, model_width)
    pair_rows = jnp.concatenate([both_rows, swap_cores(both_rows)], axis=1)
    received = pair_rows[0]
    grad_rows = pair_rows[1]
    act_gate = jnp.dot(received, gate_own, preferred_element_type=jnp.float32)
    act_up = jnp.dot(received, up_own, preferred_element_type=jnp.float32)
    sigmoid_gate = jax.nn.sigmoid(act_gate)
    silu_gate = act_gate * sigmoid_gate
    hidden = (silu_gate * act_up).astype(jnp.bfloat16)
    hidden_grad = jnp.dot(grad_rows, down_own, preferred_element_type=jnp.float32)
    gate_delta = (
        hidden_grad * act_up * sigmoid_gate * (1.0 + act_gate * (1.0 - sigmoid_gate))
    ).astype(jnp.bfloat16)
    up_delta = (hidden_grad * silu_gate).astype(jnp.bfloat16)
    grad_gate, grad_up, grad_down = scatter_grads(
        contract_first(received, gate_delta),
        contract_first(received, up_delta),
        contract_first(grad_rows, hidden),
    )
    expert_out = pair_total(contract_last(hidden, down_own), slot_count)
    token_grad = pair_total(
        contract_last(gate_delta, gate_own) + contract_last(up_delta, up_own), slot_count
    )
    back = lax.all_to_all(
        jnp.stack([expert_out, token_grad]).reshape(2, experts, capacity, model_width),
        "expert",
        split_axis=1,
        concat_axis=1,
        tiled=True,
    ).reshape(2, slot_count, model_width)
    moe_out = (gate_weight * jnp.take(back[0], slot_index, axis=0).astype(jnp.float32)).astype(
        jnp.bfloat16
    )
    grad_tokens = jnp.take(back[1], slot_index, axis=0)
    return (moe_out, grad_tokens, grad_gate[None], grad_up[None], grad_down[None])


def solution(mesh):
    dp_size, expert_size = mesh.devices.shape
    chips = dp_size // 2
    x_size = 4 if chips % 4 == 0 else 1
    grid = mesh.devices.reshape(x_size, chips // x_size, 2, expert_size)
    fine = Mesh(grid, DP + ("expert",))
    rows = P(DP + ("expert",), None)
    weights = P("expert", DP, None)
    in_specs = (rows, rows, rows, weights, weights, weights, rows)
    out_specs = (rows, rows, weights, weights, weights)
    return jax.shard_map(shards, mesh=fine, in_specs=in_specs, out_specs=out_specs, check_vma=False)
```

```python
import jax
import jax.numpy as jnp
from jax import lax
from jax.sharding import Mesh
from jax.sharding import PartitionSpec as P

TOP = 1
CHIPS = ("x", "zh")
DP = ("x", "zh", "core")


def contract_last(matrix_a, matrix_b):
    return lax.dot_general(
        matrix_a, matrix_b, (((1,), (1,)), ((), ())), preferred_element_type=jnp.float32
    )


def contract_first(matrix_a, matrix_b):
    return lax.dot_general(
        matrix_a, matrix_b, (((0,), (0,)), ((), ())), preferred_element_type=jnp.float32
    )


def swap_cores(value):
    return lax.ppermute(value, "core", perm=[(0, 1), (1, 0)])


def gather_weights(*weights):
    half = weights[0].shape[1] // 2
    first = lax.axis_index("core") == 0
    kept = jnp.stack([jnp.where(first, w[:, :half], w[:, half:]) for w in weights])
    sent = jnp.stack([jnp.where(first, w[:, half:], w[:, :half]) for w in weights])
    came = swap_cores(sent)
    own = jnp.where(
        first, jnp.concatenate([kept, came], axis=1), jnp.concatenate([came, kept], axis=1)
    )
    own = lax.all_gather(own, CHIPS, axis=1, tiled=True)
    return [own[i] for i in range(len(weights))]


def scatter_grads(parts, count):
    chip_sum = lax.psum_scatter(parts.astype(jnp.bfloat16), CHIPS, scatter_dimension=0, tiled=True)
    first = lax.axis_index("core") == 0
    rows = chip_sum.shape[0] // 2

    def my_rows(value):
        return jnp.where(first, value[:rows], value[rows:]).astype(jnp.float32)

    mine = my_rows(chip_sum)
    theirs = my_rows(swap_cores(chip_sum))
    half = parts.shape[1] // count
    blocks = []
    for i in range(count):
        a = mine[:, i * half:(i + 1) * half]
        b = theirs[:, i * half:(i + 1) * half]
        blocks.append(jnp.where(first, jnp.concatenate([a, b], axis=1), jnp.concatenate([b, a], axis=1)))
    return blocks


def pair_total(partial, slots):
    arrived = swap_cores(partial[slots:])
    return (partial[:slots] + arrived).astype(jnp.bfloat16)


def shards(tokens, routes, gate_levels, w_gate, w_up, w_down, grad_out):
    experts = lax.axis_size("expert")
    tok_rows = tokens.shape[0]
    model_width = tokens.shape[1]
    capacity = min(tok_rows, tok_rows * TOP * 5 // (4 * experts))
    slot_count = experts * capacity
    expert_of = routes[:, 0]
    onehot = (expert_of[:, None] == jnp.arange(experts, dtype=jnp.int32)[None, :]).astype(jnp.int32)
    earlier = jnp.cumsum(onehot, axis=0) - onehot
    slot_rank = jnp.sum(earlier * onehot, axis=1)
    slot_index = expert_of * capacity + slot_rank
    source_row = (
        jnp.zeros((slot_count,), jnp.int32)
        .at[slot_index]
        .set(jnp.arange(tok_rows, dtype=jnp.int32))
    )
    filled = (
        jnp.zeros((slot_count, 1), jnp.bfloat16)
        .at[slot_index, 0]
        .set(jnp.ones((tok_rows,), jnp.bfloat16))
    )
    gate_weight = gate_levels.astype(jnp.float32) / 64.0

    def pack_rows(values):
        return (jnp.take(values, source_row, axis=0) * filled).reshape(
            experts, capacity, model_width
        )

    gate_own, up_own, down_own = gather_weights(w_gate[0], w_up[0], w_down[0])
    out_grad = (gate_weight * grad_out.astype(jnp.float32)).astype(jnp.bfloat16)
    both_rows = lax.all_to_all(
        jnp.stack([pack_rows(tokens), pack_rows(out_grad)]),
        "expert",
        split_axis=1,
        concat_axis=1,
        tiled=True,
    ).reshape(2, slot_count, model_width)
    pair_rows = jnp.concatenate([both_rows, swap_cores(both_rows)], axis=1)
    received = pair_rows[0]
    grad_rows = pair_rows[1]
    act_gate = jnp.dot(received, gate_own, preferred_element_type=jnp.float32)
    act_up = jnp.dot(received, up_own, preferred_element_type=jnp.float32)
    sigmoid_gate = jax.nn.sigmoid(act_gate)
    silu_gate = act_gate * sigmoid_gate
    hidden = (silu_gate * act_up).astype(jnp.bfloat16)
    hidden_grad = jnp.dot(grad_rows, down_own, preferred_element_type=jnp.float32)
    gate_delta = (
        hidden_grad * act_up * sigmoid_gate * (1.0 + act_gate * (1.0 - sigmoid_gate))
    ).astype(jnp.bfloat16)
    up_delta = (hidden_grad * silu_gate).astype(jnp.bfloat16)
    empty = jnp.zeros_like(hidden)
    rights = jnp.concatenate(
        [
            jnp.concatenate([gate_delta, up_delta, empty], axis=1),
            jnp.concatenate([empty, empty, hidden], axis=1),
        ],
        axis=0,
    )
    lefts = pair_rows.reshape(-1, model_width)
    grad_gate, grad_up, grad_down = scatter_grads(contract_first(lefts, rights), 3)
    expert_out = pair_total(contract_last(hidden, down_own), slot_count).reshape(
        experts, capacity, model_width
    )
    returned = lax.all_to_all(
        expert_out, "expert", split_axis=0, concat_axis=0, tiled=True
    ).reshape(slot_count, model_width)
    moe_out = (gate_weight * jnp.take(returned, slot_index, axis=0).astype(jnp.float32)).astype(
        jnp.bfloat16
    )
    token_grad = pair_total(
        contract_last(gate_delta, gate_own) + contract_last(up_delta, up_own), slot_count
    )
    arrived = lax.all_to_all(
        token_grad.reshape(experts, capacity, model_width),
        "expert",
        split_axis=0,
        concat_axis=0,
        tiled=True,
    )
    grad_tokens = jnp.take(arrived.reshape(slot_count, model_width), slot_index, axis=0)
    return (moe_out, grad_tokens, grad_gate[None], grad_up[None], grad_down[None])


def solution(mesh):
    dp_size, expert_size = mesh.devices.shape
    chips = dp_size // 2
    x_size = 4 if chips % 4 == 0 else 1
    grid = mesh.devices.reshape(x_size, chips // x_size, 2, expert_size)
    fine = Mesh(grid, DP + ("expert",))
    rows = P(DP + ("expert",), None)
    weights = P("expert", DP, None)
    in_specs = (rows, rows, rows, weights, weights, weights, rows)
    out_specs = (rows, rows, weights, weights, weights)
    return jax.shard_map(shards, mesh=fine, in_specs=in_specs, out_specs=out_specs, check_vma=False)
```

```python
import jax
import jax.numpy as jnp
from jax import lax
from jax.sharding import Mesh
from jax.sharding import PartitionSpec as P

TOP = 1
CHIPS = ("x", "zh")
DP = ("x", "zh", "core")


def contract_last(matrix_a, matrix_b):
    return lax.dot_general(
        matrix_a, matrix_b, (((1,), (1,)), ((), ())), preferred_element_type=jnp.float32
    )


def contract_first(matrix_a, matrix_b):
    return lax.dot_general(
        matrix_a, matrix_b, (((0,), (0,)), ((), ())), preferred_element_type=jnp.float32
    )


def swap_cores(value):
    return lax.ppermute(value, "core", perm=[(0, 1), (1, 0)])


def gather_weights(*weights):
    full = lax.all_gather(jnp.stack(weights), DP, axis=1, tiled=True)
    half = full.shape[2] // 2
    first = lax.axis_index("core") == 0
    return [jnp.where(first, full[i, :, :half], full[i, :, half:]) for i in range(len(weights))]


def scatter_grads(*parts):
    stacked = jnp.stack(parts).astype(jnp.bfloat16)
    chip_sum = lax.psum_scatter(stacked, CHIPS, scatter_dimension=1, tiled=True)
    first = lax.axis_index("core") == 0
    rows = chip_sum.shape[1] // 2

    def my_rows(value):
        return jnp.where(first, value[:, :rows], value[:, rows:]).astype(jnp.float32)

    mine = my_rows(chip_sum)
    theirs = my_rows(swap_cores(chip_sum))
    block = jnp.where(
        first, jnp.concatenate([mine, theirs], axis=2), jnp.concatenate([theirs, mine], axis=2)
    )
    return [block[i] for i in range(len(parts))]


def pair_total(partial, slots):
    arrived = swap_cores(partial[slots:])
    return (partial[:slots] + arrived).astype(jnp.bfloat16)


def shards(tokens, routes, gate_levels, w_gate, w_up, w_down, grad_out):
    experts = lax.axis_size("expert")
    tok_rows = tokens.shape[0]
    model_width = tokens.shape[1]
    capacity = min(tok_rows, tok_rows * TOP * 5 // (4 * experts))
    slot_count = experts * capacity
    expert_of = routes[:, 0]
    onehot = (expert_of[:, None] == jnp.arange(experts, dtype=jnp.int32)[None, :]).astype(jnp.int32)
    earlier = jnp.cumsum(onehot, axis=0) - onehot
    slot_rank = jnp.sum(earlier * onehot, axis=1)
    slot_index = expert_of * capacity + slot_rank
    source_row = (
        jnp.zeros((slot_count,), jnp.int32)
        .at[slot_index]
        .set(jnp.arange(tok_rows, dtype=jnp.int32))
    )
    filled = (
        jnp.zeros((slot_count, 1), jnp.bfloat16)
        .at[slot_index, 0]
        .set(jnp.ones((tok_rows,), jnp.bfloat16))
    )
    gate_weight = gate_levels.astype(jnp.float32) / 64.0

    def pack_rows(values):
        return (jnp.take(values, source_row, axis=0) * filled).reshape(
            experts, capacity, model_width
        )

    gate_own, up_own, down_own = gather_weights(w_gate[0], w_up[0], w_down[0])
    out_grad = (gate_weight * grad_out.astype(jnp.float32)).astype(jnp.bfloat16)
    both_rows = lax.all_to_all(
        jnp.stack([pack_rows(tokens), pack_rows(out_grad)]),
        "expert",
        split_axis=1,
        concat_axis=1,
        tiled=True,
    ).reshape(2, slot_count, model_width)
    pair_rows = jnp.concatenate([both_rows, swap_cores(both_rows)], axis=1)
    received = pair_rows[0]
    grad_rows = pair_rows[1]
    act_gate = jnp.dot(received, gate_own, preferred_element_type=jnp.float32)
    act_up = jnp.dot(received, up_own, preferred_element_type=jnp.float32)
    sigmoid_gate = jax.nn.sigmoid(act_gate)
    silu_gate = act_gate * sigmoid_gate
    hidden = (silu_gate * act_up).astype(jnp.bfloat16)
    hidden_grad = jnp.dot(grad_rows, down_own, preferred_element_type=jnp.float32)
    gate_delta = (
        hidden_grad * act_up * sigmoid_gate * (1.0 + act_gate * (1.0 - sigmoid_gate))
    ).astype(jnp.bfloat16)
    up_delta = (hidden_grad * silu_gate).astype(jnp.bfloat16)
    grad_gate, grad_up, grad_down = scatter_grads(
        contract_first(received, gate_delta),
        contract_first(received, up_delta),
        contract_first(grad_rows, hidden),
    )
    expert_out = pair_total(contract_last(hidden, down_own), slot_count).reshape(
        experts, capacity, model_width
    )
    returned = lax.all_to_all(
        expert_out, "expert", split_axis=0, concat_axis=0, tiled=True
    ).reshape(slot_count, model_width)
    moe_out = (gate_weight * jnp.take(returned, slot_index, axis=0).astype(jnp.float32)).astype(
        jnp.bfloat16
    )
    token_grad = pair_total(
        contract_last(gate_delta, gate_own) + contract_last(up_delta, up_own), slot_count
    )
    arrived = lax.all_to_all(
        token_grad.reshape(experts, capacity, model_width),
        "expert",
        split_axis=0,
        concat_axis=0,
        tiled=True,
    )
    grad_tokens = jnp.take(arrived.reshape(slot_count, model_width), slot_index, axis=0)
    return (moe_out, grad_tokens, grad_gate[None], grad_up[None], grad_down[None])


def solution(mesh):
    dp_size, expert_size = mesh.devices.shape
    chips = dp_size // 2
    x_size = 4 if chips % 4 == 0 else 1
    grid = mesh.devices.reshape(x_size, chips // x_size, 2, expert_size)
    fine = Mesh(grid, DP + ("expert",))
    rows = P(DP + ("expert",), None)
    weights = P("expert", DP, None)
    in_specs = (rows, rows, rows, weights, weights, weights, rows)
    out_specs = (rows, rows, weights, weights, weights)
    return jax.shard_map(shards, mesh=fine, in_specs=in_specs, out_specs=out_specs, check_vma=False)
```

```python
import jax
import jax.numpy as jnp
from jax import lax
from jax.sharding import Mesh
from jax.sharding import PartitionSpec as P

TOP = 1
CHIPS = ("x", "zh")
DP = ("x", "zh", "core")


def contract_last(matrix_a, matrix_b):
    return lax.dot_general(
        matrix_a, matrix_b, (((1,), (1,)), ((), ())), preferred_element_type=jnp.float32
    )


def contract_first(matrix_a, matrix_b):
    return lax.dot_general(
        matrix_a, matrix_b, (((0,), (0,)), ((), ())), preferred_element_type=jnp.float32
    )


def swap_cores(value):
    return lax.ppermute(value, "core", perm=[(0, 1), (1, 0)])


def gather_weights(*weights):
    full = lax.all_gather(jnp.stack(weights), DP, axis=1, tiled=True)
    half = full.shape[2] // 2
    start = lax.axis_index("core") * half
    return [lax.dynamic_slice_in_dim(full[i], start, half, axis=1) for i in range(len(weights))]


def scatter_grads(*parts):
    stacked = jnp.stack(parts).astype(jnp.bfloat16)
    chip_sum = lax.psum_scatter(stacked, CHIPS, scatter_dimension=1, tiled=True)
    first = lax.axis_index("core") == 0
    rows = chip_sum.shape[1] // 2

    def my_rows(value):
        return jnp.where(first, value[:, :rows], value[:, rows:]).astype(jnp.float32)

    mine = my_rows(chip_sum)
    theirs = my_rows(swap_cores(chip_sum))
    block = jnp.where(
        first, jnp.concatenate([mine, theirs], axis=2), jnp.concatenate([theirs, mine], axis=2)
    )
    return [block[i] for i in range(len(parts))]


def pair_total(partial, slots):
    arrived = swap_cores(partial[slots:])
    return (partial[:slots] + arrived).astype(jnp.bfloat16)


def shards(tokens, routes, gate_levels, w_gate, w_up, w_down, grad_out):
    experts = lax.axis_size("expert")
    tok_rows = tokens.shape[0]
    model_width = tokens.shape[1]
    capacity = min(tok_rows, tok_rows * TOP * 5 // (4 * experts))
    slot_count = experts * capacity
    expert_of = routes[:, 0]
    onehot = (expert_of[:, None] == jnp.arange(experts, dtype=jnp.int32)[None, :]).astype(jnp.int32)
    earlier = jnp.cumsum(onehot, axis=0) - onehot
    slot_rank = jnp.sum(earlier * onehot, axis=1)
    slot_index = expert_of * capacity + slot_rank
    source_row = (
        jnp.zeros((slot_count,), jnp.int32)
        .at[slot_index]
        .set(jnp.arange(tok_rows, dtype=jnp.int32))
    )
    filled = (
        jnp.zeros((slot_count, 1), jnp.bfloat16)
        .at[slot_index, 0]
        .set(jnp.ones((tok_rows,), jnp.bfloat16))
    )
    gate_weight = gate_levels.astype(jnp.float32) / 64.0

    def pack_rows(values):
        return (jnp.take(values, source_row, axis=0) * filled).reshape(
            experts, capacity, model_width
        )

    gate_own, up_own, down_own = gather_weights(w_gate[0], w_up[0], w_down[0])
    out_grad = (gate_weight * grad_out.astype(jnp.float32)).astype(jnp.bfloat16)
    both_rows = lax.all_to_all(
        jnp.stack([pack_rows(tokens), pack_rows(out_grad)]),
        "expert",
        split_axis=1,
        concat_axis=1,
        tiled=True,
    ).reshape(2, slot_count, model_width)
    pair_rows = jnp.concatenate([both_rows, swap_cores(both_rows)], axis=1)
    received = pair_rows[0]
    grad_rows = pair_rows[1]
    act_gate = jnp.dot(received, gate_own, preferred_element_type=jnp.float32)
    act_up = jnp.dot(received, up_own, preferred_element_type=jnp.float32)
    sigmoid_gate = jax.nn.sigmoid(act_gate)
    silu_gate = act_gate * sigmoid_gate
    hidden = (silu_gate * act_up).astype(jnp.bfloat16)
    hidden_grad = jnp.dot(grad_rows, down_own, preferred_element_type=jnp.float32)
    gate_delta = (
        hidden_grad * act_up * sigmoid_gate * (1.0 + act_gate * (1.0 - sigmoid_gate))
    ).astype(jnp.bfloat16)
    up_delta = (hidden_grad * silu_gate).astype(jnp.bfloat16)
    grad_gate, grad_up, grad_down = scatter_grads(
        contract_first(received, gate_delta),
        contract_first(received, up_delta),
        contract_first(grad_rows, hidden),
    )
    expert_out = pair_total(contract_last(hidden, down_own), slot_count).reshape(
        experts, capacity, model_width
    )
    returned = lax.all_to_all(
        expert_out, "expert", split_axis=0, concat_axis=0, tiled=True
    ).reshape(slot_count, model_width)
    moe_out = (gate_weight * jnp.take(returned, slot_index, axis=0).astype(jnp.float32)).astype(
        jnp.bfloat16
    )
    token_grad = pair_total(
        contract_last(gate_delta, gate_own) + contract_last(up_delta, up_own), slot_count
    )
    arrived = lax.all_to_all(
        token_grad.reshape(experts, capacity, model_width),
        "expert",
        split_axis=0,
        concat_axis=0,
        tiled=True,
    )
    grad_tokens = jnp.take(arrived.reshape(slot_count, model_width), slot_index, axis=0)
    return (moe_out, grad_tokens, grad_gate[None], grad_up[None], grad_down[None])


def solution(mesh):
    dp_size, expert_size = mesh.devices.shape
    chips = dp_size // 2
    x_size = 4 if chips % 4 == 0 else 1
    grid = mesh.devices.reshape(x_size, chips // x_size, 2, expert_size)
    fine = Mesh(grid, DP + ("expert",))
    rows = P(DP + ("expert",), None)
    weights = P("expert", DP, None)
    in_specs = (rows, rows, rows, weights, weights, weights, rows)
    out_specs = (rows, rows, weights, weights, weights)
    return jax.shard_map(shards, mesh=fine, in_specs=in_specs, out_specs=out_specs, check_vma=False)
```

```python
import jax
import jax.numpy as jnp
from jax import lax
from jax.sharding import Mesh
from jax.sharding import PartitionSpec as P

TOP = 1
CHIPS = ("x", "zh")
DP = ("x", "zh", "core")


def contract_last(matrix_a, matrix_b):
    return lax.dot_general(
        matrix_a, matrix_b, (((1,), (1,)), ((), ())), preferred_element_type=jnp.float32
    )


def contract_first(matrix_a, matrix_b):
    return lax.dot_general(
        matrix_a, matrix_b, (((0,), (0,)), ((), ())), preferred_element_type=jnp.float32
    )


def swap_cores(value):
    return lax.ppermute(value, "core", perm=[(0, 1), (1, 0)])


def gather_weights(*weights):
    half = weights[0].shape[1] // 2
    first = lax.axis_index("core") == 0
    kept = jnp.stack([jnp.where(first, w[:, :half], w[:, half:]) for w in weights])
    sent = jnp.stack([jnp.where(first, w[:, half:], w[:, :half]) for w in weights])
    came = swap_cores(sent)
    own = jnp.where(
        first, jnp.concatenate([kept, came], axis=1), jnp.concatenate([came, kept], axis=1)
    )
    own = lax.all_gather(own, CHIPS, axis=1, tiled=True)
    return [own[i] for i in range(len(weights))]


def scatter_grads(*parts):
    stacked = jnp.stack(parts).astype(jnp.bfloat16)
    chip_sum = lax.psum_scatter(stacked, CHIPS, scatter_dimension=1, tiled=True)
    first = lax.axis_index("core") == 0
    rows = chip_sum.shape[1] // 2

    def my_rows(value):
        return jnp.where(first, value[:, :rows], value[:, rows:]).astype(jnp.float32)

    mine = my_rows(chip_sum)
    theirs = my_rows(swap_cores(chip_sum))
    block = jnp.where(
        first, jnp.concatenate([mine, theirs], axis=2), jnp.concatenate([theirs, mine], axis=2)
    )
    return [block[i] for i in range(len(parts))]


def pair_total(partial, slots):
    arrived = swap_cores(partial[slots:].astype(jnp.bfloat16))
    return (partial[:slots] + arrived.astype(jnp.float32)).astype(jnp.bfloat16)


def shards(tokens, routes, gate_levels, w_gate, w_up, w_down, grad_out):
    experts = lax.axis_size("expert")
    tok_rows = tokens.shape[0]
    model_width = tokens.shape[1]
    capacity = min(tok_rows, tok_rows * TOP * 5 // (4 * experts))
    slot_count = experts * capacity
    expert_of = routes[:, 0]
    onehot = (expert_of[:, None] == jnp.arange(experts, dtype=jnp.int32)[None, :]).astype(jnp.int32)
    earlier = jnp.cumsum(onehot, axis=0) - onehot
    slot_rank = jnp.sum(earlier * onehot, axis=1)
    slot_index = expert_of * capacity + slot_rank
    source_row = (
        jnp.zeros((slot_count,), jnp.int32)
        .at[slot_index]
        .set(jnp.arange(tok_rows, dtype=jnp.int32))
    )
    filled = (
        jnp.zeros((slot_count, 1), jnp.bfloat16)
        .at[slot_index, 0]
        .set(jnp.ones((tok_rows,), jnp.bfloat16))
    )
    gate_weight = gate_levels.astype(jnp.float32) / 64.0

    def pack_rows(values):
        return (jnp.take(values, source_row, axis=0) * filled).reshape(
            experts, capacity, model_width
        )

    gate_own, up_own, down_own = gather_weights(w_gate[0], w_up[0], w_down[0])
    out_grad = (gate_weight * grad_out.astype(jnp.float32)).astype(jnp.bfloat16)
    both_rows = lax.all_to_all(
        jnp.stack([pack_rows(tokens), pack_rows(out_grad)]),
        "expert",
        split_axis=1,
        concat_axis=1,
        tiled=True,
    ).reshape(2, slot_count, model_width)
    pair_rows = jnp.concatenate([both_rows, swap_cores(both_rows)], axis=1)
    received = pair_rows[0]
    grad_rows = pair_rows[1]
    act_gate = jnp.dot(received, gate_own, preferred_element_type=jnp.float32)
    act_up = jnp.dot(received, up_own, preferred_element_type=jnp.float32)
    sigmoid_gate = jax.nn.sigmoid(act_gate)
    silu_gate = act_gate * sigmoid_gate
    hidden = (silu_gate * act_up).astype(jnp.bfloat16)
    hidden_grad = jnp.dot(grad_rows, down_own, preferred_element_type=jnp.float32)
    gate_delta = (
        hidden_grad * act_up * sigmoid_gate * (1.0 + act_gate * (1.0 - sigmoid_gate))
    ).astype(jnp.bfloat16)
    up_delta = (hidden_grad * silu_gate).astype(jnp.bfloat16)
    grad_gate, grad_up, grad_down = scatter_grads(
        contract_first(received, gate_delta),
        contract_first(received, up_delta),
        contract_first(grad_rows, hidden),
    )
    expert_out = pair_total(contract_last(hidden, down_own), slot_count).reshape(
        experts, capacity, model_width
    )
    returned = lax.all_to_all(
        expert_out, "expert", split_axis=0, concat_axis=0, tiled=True
    ).reshape(slot_count, model_width)
    moe_out = (gate_weight * jnp.take(returned, slot_index, axis=0).astype(jnp.float32)).astype(
        jnp.bfloat16
    )
    token_grad = pair_total(
        contract_last(gate_delta, gate_own) + contract_last(up_delta, up_own), slot_count
    )
    arrived = lax.all_to_all(
        token_grad.reshape(experts, capacity, model_width),
        "expert",
        split_axis=0,
        concat_axis=0,
        tiled=True,
    )
    grad_tokens = jnp.take(arrived.reshape(slot_count, model_width), slot_index, axis=0)
    return (moe_out, grad_tokens, grad_gate[None], grad_up[None], grad_down[None])


def solution(mesh):
    dp_size, expert_size = mesh.devices.shape
    chips = dp_size // 2
    x_size = 4 if chips % 4 == 0 else 1
    grid = mesh.devices.reshape(x_size, chips // x_size, 2, expert_size)
    fine = Mesh(grid, DP + ("expert",))
    rows = P(DP + ("expert",), None)
    weights = P("expert", DP, None)
    in_specs = (rows, rows, rows, weights, weights, weights, rows)
    out_specs = (rows, rows, weights, weights, weights)
    return jax.shard_map(shards, mesh=fine, in_specs=in_specs, out_specs=out_specs, check_vma=False)
```

```python
import jax
import jax.numpy as jnp
from jax import lax
from jax.sharding import Mesh
from jax.sharding import PartitionSpec as P

TOP = 1
CHIPS = ("x", "zh")
DP = ("x", "zh", "core")


def contract_last(matrix_a, matrix_b):
    return lax.dot_general(
        matrix_a, matrix_b, (((1,), (1,)), ((), ())), preferred_element_type=jnp.float32
    )


def contract_first(matrix_a, matrix_b):
    return lax.dot_general(
        matrix_a, matrix_b, (((0,), (0,)), ((), ())), preferred_element_type=jnp.float32
    )


def swap_cores(value):
    return lax.ppermute(value, "core", perm=[(0, 1), (1, 0)])


def gather_weights(*weights):
    half = weights[0].shape[1] // 2
    first = lax.axis_index("core") == 0
    kept = jnp.stack([jnp.where(first, w[:, :half], w[:, half:]) for w in weights])
    sent = jnp.stack([jnp.where(first, w[:, half:], w[:, :half]) for w in weights])
    came = swap_cores(sent)
    own = jnp.where(
        first, jnp.concatenate([kept, came], axis=1), jnp.concatenate([came, kept], axis=1)
    )
    own = lax.all_gather(own, CHIPS, axis=1, tiled=True)
    return [own[i] for i in range(len(weights))]


def scatter_grads(*parts):
    stacked = jnp.stack(parts).astype(jnp.bfloat16)
    chip_sum = lax.psum_scatter(stacked, CHIPS, scatter_dimension=1, tiled=True)
    first = lax.axis_index("core") == 0
    rows = chip_sum.shape[1] // 2

    def my_rows(value):
        return jnp.where(first, value[:, :rows], value[:, rows:]).astype(jnp.float32)

    mine = my_rows(chip_sum)
    sent = jnp.where(first, chip_sum[:, rows:], chip_sum[:, :rows])
    theirs = swap_cores(sent).astype(jnp.float32)
    block = jnp.where(
        first, jnp.concatenate([mine, theirs], axis=2), jnp.concatenate([theirs, mine], axis=2)
    )
    return [block[i] for i in range(len(parts))]


def pair_total(partial, slots):
    arrived = swap_cores(partial[slots:].astype(jnp.bfloat16))
    return (partial[:slots] + arrived.astype(jnp.float32)).astype(jnp.bfloat16)


def shards(tokens, routes, gate_levels, w_gate, w_up, w_down, grad_out):
    experts = lax.axis_size("expert")
    tok_rows = tokens.shape[0]
    model_width = tokens.shape[1]
    capacity = min(tok_rows, tok_rows * TOP * 5 // (4 * experts))
    slot_count = experts * capacity
    expert_of = routes[:, 0]
    onehot = (expert_of[:, None] == jnp.arange(experts, dtype=jnp.int32)[None, :]).astype(jnp.int32)
    earlier = jnp.cumsum(onehot, axis=0) - onehot
    slot_rank = jnp.sum(earlier * onehot, axis=1)
    slot_index = expert_of * capacity + slot_rank
    source_row = (
        jnp.zeros((slot_count,), jnp.int32)
        .at[slot_index]
        .set(jnp.arange(tok_rows, dtype=jnp.int32))
    )
    filled = (
        jnp.zeros((slot_count, 1), jnp.bfloat16)
        .at[slot_index, 0]
        .set(jnp.ones((tok_rows,), jnp.bfloat16))
    )
    gate_weight = gate_levels.astype(jnp.float32) / 64.0

    def pack_rows(values):
        return (jnp.take(values, source_row, axis=0) * filled).reshape(
            experts, capacity, model_width
        )

    gate_own, up_own, down_own = gather_weights(w_gate[0], w_up[0], w_down[0])
    out_grad = (gate_weight * grad_out.astype(jnp.float32)).astype(jnp.bfloat16)
    both_rows = lax.all_to_all(
        jnp.stack([pack_rows(tokens), pack_rows(out_grad)]),
        "expert",
        split_axis=1,
        concat_axis=1,
        tiled=True,
    ).reshape(2, slot_count, model_width)
    pair_rows = jnp.concatenate([both_rows, swap_cores(both_rows)], axis=1)
    received = pair_rows[0]
    grad_rows = pair_rows[1]
    act_gate = jnp.dot(received, gate_own, preferred_element_type=jnp.float32)
    act_up = jnp.dot(received, up_own, preferred_element_type=jnp.float32)
    sigmoid_gate = jax.nn.sigmoid(act_gate)
    silu_gate = act_gate * sigmoid_gate
    hidden = (silu_gate * act_up).astype(jnp.bfloat16)
    hidden_grad = jnp.dot(grad_rows, down_own, preferred_element_type=jnp.float32)
    gate_delta = (
        hidden_grad * act_up * sigmoid_gate * (1.0 + act_gate * (1.0 - sigmoid_gate))
    ).astype(jnp.bfloat16)
    up_delta = (hidden_grad * silu_gate).astype(jnp.bfloat16)
    grad_gate, grad_up, grad_down = scatter_grads(
        contract_first(received, gate_delta),
        contract_first(received, up_delta),
        contract_first(grad_rows, hidden),
    )
    expert_out = pair_total(contract_last(hidden, down_own), slot_count).reshape(
        experts, capacity, model_width
    )
    returned = lax.all_to_all(
        expert_out, "expert", split_axis=0, concat_axis=0, tiled=True
    ).reshape(slot_count, model_width)
    moe_out = (gate_weight * jnp.take(returned, slot_index, axis=0).astype(jnp.float32)).astype(
        jnp.bfloat16
    )
    token_grad = pair_total(
        contract_last(gate_delta, gate_own) + contract_last(up_delta, up_own), slot_count
    )
    arrived = lax.all_to_all(
        token_grad.reshape(experts, capacity, model_width),
        "expert",
        split_axis=0,
        concat_axis=0,
        tiled=True,
    )
    grad_tokens = jnp.take(arrived.reshape(slot_count, model_width), slot_index, axis=0)
    return (moe_out, grad_tokens, grad_gate[None], grad_up[None], grad_down[None])


def solution(mesh):
    dp_size, expert_size = mesh.devices.shape
    chips = dp_size // 2
    x_size = 4 if chips % 4 == 0 else 1
    grid = mesh.devices.reshape(x_size, chips // x_size, 2, expert_size)
    fine = Mesh(grid, DP + ("expert",))
    rows = P(DP + ("expert",), None)
    weights = P("expert", DP, None)
    in_specs = (rows, rows, rows, weights, weights, weights, rows)
    out_specs = (rows, rows, weights, weights, weights)
    return jax.shard_map(shards, mesh=fine, in_specs=in_specs, out_specs=out_specs, check_vma=False)
```
